768 devices in a mesh: vert: 24 (over z, core), feat: 32 (over y, x).
Axes of the slice: x: 4, y: 8, z: 12, core: 2. Of those that a mesh axis runs over, the one named last changes fastest.
Arguments:
- states: bfloat16 [4, 256, 98304], P(None, 'feat', 'vert'), may hold values from -6 to 6
- depth_weight: float32 [4, 256], P(None, 'feat'), may hold values from -1 to 1
- tile_values: bfloat16 [24, 256, 128, 128], P('vert'), may hold values from -0.1875 to 0.1875
- tile_dst: int32 [24, 256], P('vert'), may hold values from 0 to 31
- tile_src: int32 [24, 256], P('vert'), may hold values from 0 to 43
- tile_count: int32 [24], P('vert'), may hold values from 64 to 256, as said below
- send_rows: int32 [24, 24, 64], P('vert'), may hold values from 0 to 4095
- weight: bfloat16 [256, 256], replicated, may hold values from -0.375 to 0.375
- bias_vec: float32 [256], P('feat'), may hold values from -3 to 3
- cotangent: bfloat16 [256, 98304], P('feat', 'vert'), may hold values from -6 to 6
Outputs:
- layer_out: bfloat16 [256, 98304], P('feat', 'vert')
- grad_states: bfloat16 [4, 256, 98304], P(None, 'feat', 'vert')
- grad_weight: float32 [256, 256], P('feat')
- grad_bias: float32 [256], P('feat')
- grad_depth: float32 [4, 256], P(None, 'feat')
The draws below stay inside these ranges and needn't reach their ends.
Inputs may be any that keep to these rules, and one draw needn't show every extreme that they name: `tile_count`: at least 64 tiles in every partition, and exactly 256 in some partition.
All inputs are finite; a program needn't handle non-finite values.
Results may differ from the reference program's by a relative error of at most 0.024.
Values may be sent and summed in bfloat16 or wider, within the bound.
No kernel may reach another device: no remote copies, remote signals or barrier semaphores. Data moves between devices by JAX's collectives and lax.ppermute only.
A program may use at most 64 MiB of HBM per device.

```python
import math
import jax
import jax.numpy as jnp
from jax import lax

D = 256
STATES = 4
BLOCK = 128
HALO = 64
ROWS = 4096
SECTIONS = 24
TILE_CAP = 256
VERTICES = 98304


def draw_tile_count(key, part):
    first_key, second_key = jax.random.split(jax.random.fold_in(key, 7))
    counts = jax.random.randint(first_key, (SECTIONS,), TILE_CAP // 4, TILE_CAP + 1, dtype=jnp.int32)
    fullest = jax.random.randint(second_key, (), 0, SECTIONS, dtype=jnp.int32)
    return jnp.where(jnp.arange(SECTIONS, dtype=jnp.int32) == fullest, jnp.int32(TILE_CAP), counts).astype(jnp.int32)


def set_ends(drawn, own_key, smallest, top_value):
    longest = drawn.shape.index(max(drawn.shape))
    spots = []
    for shift in (0, 1):
        where = [jax.random.randint(jax.random.fold_in(own_key, axis), (), 0, length) for axis, length in enumerate(drawn.shape)]
        where[longest] = (where[longest] + shift) % drawn.shape[longest]
        spots.append(tuple(where))
    return drawn.at[spots[0]].set(smallest).at[spots[1]].set(top_value)


def level_of(stream_key, dims, cuts, smallest, largest):
    loudness, own = 1.0, jax.random.fold_in(stream_key, 6)
    for dim, shards_of in cuts:
        draws = jnp.exp(jax.random.uniform(jax.random.fold_in(own, dim), (shards_of,), jnp.float32, smallest / len(cuts), largest / len(cuts)))
        loudness = loudness * jnp.repeat(draws, dims[dim] // shards_of).reshape([-1 if axis == dim else 1 for axis in range(len(dims))])
    return loudness


def bell_draw(stream_key, dims, width, limit, cuts=(), held_as=jnp.bfloat16):
    gain = level_of(stream_key, dims, cuts, -0.22, 0.18) if cuts else 1.0
    entries = jax.random.normal(stream_key, dims, jnp.float32) * width * gain
    return jnp.minimum(jnp.maximum(entries, -limit), limit).astype(held_as)


def setup_inputs(seed: int = 0) -> dict:
    key_list = jax.random.split(jax.random.key(seed), 11)
    states = bell_draw(key_list[0], (STATES, D, VERTICES), 1.0, 6.0, ((1, 32), (2, 24)))
    depth_weight = jnp.clip(jax.random.uniform(key_list[1], (STATES, D), jnp.float32, -1.0, 1.0) * level_of(key_list[1], (STATES, D), ((1, 32),), -0.4, 0.0), -1.0, 1.0)
    tile_values = bell_draw(key_list[2], (SECTIONS, TILE_CAP, BLOCK, BLOCK), (8 * BLOCK) ** -0.5, 0.1875, ((0, 24),))
    tile_dst = set_ends(jax.random.randint(key_list[3], (SECTIONS, TILE_CAP), 0, ROWS // BLOCK), jax.random.fold_in(key_list[3], 1), 0, (ROWS // BLOCK) - 1).astype(jnp.int32)
    tile_src = set_ends(jax.random.randint(key_list[4], (SECTIONS, TILE_CAP), 0, (ROWS + SECTIONS * HALO) // BLOCK), jax.random.fold_in(key_list[4], 1), 0, ((ROWS + SECTIONS * HALO) // BLOCK) - 1).astype(jnp.int32)
    tile_count = draw_tile_count(jax.random.fold_in(key_list[10], 71), 0)
    send_rows = set_ends(jax.random.randint(key_list[6], (SECTIONS, SECTIONS, HALO), 0, ROWS), jax.random.fold_in(key_list[6], 1), 0, ROWS - 1).astype(jnp.int32)
    weight = bell_draw(key_list[7], (D, D), D ** -0.5, 0.375)
    bias_vec = bell_draw(key_list[8], (D,), 0.5, 3.0, ((0, 32),), jnp.float32)
    cotangent = bell_draw(key_list[9], (D, VERTICES), 1.0, 6.0, ((0, 32), (1, 24)))
    return dict(states=states, depth_weight=depth_weight, tile_values=tile_values, tile_dst=tile_dst, tile_src=tile_src, tile_count=tile_count, send_rows=send_rows, weight=weight, bias_vec=bias_vec, cotangent=cotangent)


def halo_columns(send_rows, section):
    base = jnp.arange(SECTIONS, dtype=jnp.int32)[:, None] * ROWS
    return (base + send_rows[:, section, :]).reshape(-1).astype(jnp.int32)

def aggregate(mixed_state, tile_values, tile_dst, tile_src, tile_count, send_rows):
    row_blocks = ROWS // BLOCK
    src_blocks = (ROWS + SECTIONS * HALO) // BLOCK

    def one_part(section):
        local_part = lax.dynamic_slice_in_dim(mixed_state, (section * ROWS).astype(jnp.int32), ROWS, 1)
        halo_part = jnp.take(mixed_state, halo_columns(send_rows, section), axis=1)
        extended = jnp.concatenate([local_part, halo_part], axis=1).reshape(D, src_blocks, BLOCK)
        picked = jnp.take(extended, tile_src[section], axis=1).astype(jnp.float32)
        products = jnp.einsum('dtc,trc->dtr', picked, tile_values[section].astype(jnp.float32))
        live_mask = jnp.arange(TILE_CAP, dtype=jnp.int32) < tile_count[section]
        onehot = ((tile_dst[section][:, None] == jnp.arange(row_blocks, dtype=jnp.int32)[None, :]) & live_mask[:, None]).astype(jnp.float32)
        return jnp.einsum('dtr,tn->dnr', products, onehot).reshape(D, ROWS)
    parted = lax.map(one_part, jnp.arange(SECTIONS, dtype=jnp.int32))
    return jnp.transpose(parted, (1, 0, 2)).reshape(D, SECTIONS * ROWS)

def spread(grad_agg, tile_values, tile_dst, tile_src, tile_count, send_rows):
    row_blocks = ROWS // BLOCK
    src_blocks = (ROWS + SECTIONS * HALO) // BLOCK

    def one_part(running, section):
        start_col = (section * ROWS).astype(jnp.int32)
        local_grad = lax.dynamic_slice_in_dim(grad_agg, start_col, ROWS, 1).reshape(D, row_blocks, BLOCK)
        picked = jnp.take(local_grad, tile_dst[section], axis=1).astype(jnp.float32)
        products = jnp.einsum('dtr,trc->dtc', picked, tile_values[section].astype(jnp.float32))
        live_mask = jnp.arange(TILE_CAP, dtype=jnp.int32) < tile_count[section]
        onehot = ((tile_src[section][:, None] == jnp.arange(src_blocks, dtype=jnp.int32)[None, :]) & live_mask[:, None]).astype(jnp.float32)
        extended = jnp.einsum('dtc,ts->dsc', products, onehot).reshape(D, src_blocks * BLOCK)
        halo_terms = lax.optimization_barrier(extended[:, ROWS:].astype(jnp.bfloat16)).astype(jnp.float32)
        own_now = lax.dynamic_slice_in_dim(running, start_col, ROWS, 1)
        running = lax.dynamic_update_slice_in_dim(running, own_now + extended[:, :ROWS], start_col, 1)
        running = running.at[:, halo_columns(send_rows, section)].add(halo_terms)
        return (running, None)
    start = jnp.zeros((D, SECTIONS * ROWS), jnp.float32)
    result, unused = lax.scan(one_part, start, jnp.arange(SECTIONS, dtype=jnp.int32))
    return result

def reference(states, depth_weight, tile_values, tile_dst, tile_src, tile_count, send_rows, weight, bias_vec, cotangent):
    norm_scale = 1.0 / math.sqrt(VERTICES)
    states32 = states.astype(jnp.float32)
    mixed_state = lax.optimization_barrier(jnp.sum(depth_weight[:, :, None] * states32, axis=0)).astype(jnp.bfloat16)
    aggregated = aggregate(mixed_state, tile_values, tile_dst, tile_src, tile_count, send_rows).astype(jnp.bfloat16)
    pre_act = jnp.dot(weight.T, aggregated, preferred_element_type=jnp.float32) + bias_vec[:, None]
    sigmoid_pre = jax.nn.sigmoid(pre_act)
    layer_out = (pre_act * sigmoid_pre).astype(jnp.bfloat16)
    grad_pre = (cotangent.astype(jnp.float32) * sigmoid_pre * (1.0 + pre_act * (1.0 - sigmoid_pre))).astype(jnp.bfloat16)
    grad_agg = jnp.dot(weight, grad_pre, preferred_element_type=jnp.float32).astype(jnp.bfloat16)
    grad_weight = jnp.dot(aggregated, grad_pre.T, preferred_element_type=jnp.float32) * norm_scale
    grad_bias = lax.optimization_barrier(jnp.sum(grad_pre.astype(jnp.float32), axis=1)) * norm_scale
    grad_mixed = spread(grad_agg, tile_values, tile_dst, tile_src, tile_count, send_rows)
    grad_states = (depth_weight[:, :, None] * grad_mixed[None]).astype(jnp.bfloat16)
    grad_depth = lax.optimization_barrier(jnp.sum(states32 * grad_mixed[None], axis=2)) * norm_scale
    return (layer_out, grad_states, grad_weight, grad_bias, grad_depth)
```

```python
import math

import jax
import jax.numpy as jnp
from jax import lax
from jax.sharding import PartitionSpec as P


def tile_forward(extended, tile_grp, dst_grp, src_grp, live_mask, row_blocks):
    picked = jnp.take(extended, src_grp, axis=1)
    products = jnp.einsum("dtc,trc->dtr", picked, tile_grp, preferred_element_type=jnp.float32)
    onehot = (
        (dst_grp[:, None] == jnp.arange(row_blocks, dtype=jnp.int32)[None, :]) & live_mask[:, None]
    ).astype(jnp.float32)
    return jnp.einsum("dtr,tn->dnr", products, onehot)


def tile_backward(grad_blocks, tile_grp, dst_grp, src_grp, live_mask, src_blocks):
    picked = jnp.take(grad_blocks, dst_grp, axis=1)
    products = jnp.einsum("dtr,trc->dtc", picked, tile_grp, preferred_element_type=jnp.float32)
    onehot = (
        (src_grp[:, None] == jnp.arange(src_blocks, dtype=jnp.int32)[None, :]) & live_mask[:, None]
    ).astype(jnp.float32)
    return jnp.einsum("dtc,ts->dsc", products, onehot)


def over_tiles(kernel, source, tile_values, tile_dst, tile_src, tile_total, out_blocks):
    capacity = tile_values.shape[0]
    live_mask = jnp.arange(capacity, dtype=jnp.int32) < tile_total
    return kernel(source, tile_values, tile_dst, tile_src, live_mask, out_blocks)


def to_vertex_split(panel):
    return lax.all_to_all(panel, "feat", split_axis=1, concat_axis=0, tiled=True)


def to_channel_split(block):
    return lax.all_to_all(block, "feat", split_axis=0, concat_axis=1, tiled=True)


def local(
    states,
    depth_weight,
    tile_values,
    tile_dst,
    tile_src,
    tile_count,
    send_rows,
    weight,
    bias_vec,
    cotangent,
):
    channels = states.shape[1]
    row_count = states.shape[2]
    block_size = tile_values.shape[2]
    row_blocks = row_count // block_size
    my_tiles = tile_values[0]
    my_dst = tile_dst[0]
    my_src = tile_src[0]
    tile_total = tile_count[0]
    my_send = send_rows[0]
    section_count = my_send.shape[0]
    halo_width = my_send.shape[1]
    vert_count = lax.axis_size("vert")
    src_blocks = (row_count + section_count * halo_width) // block_size
    norm_scale = 1.0 / math.sqrt(vert_count * row_count)
    cot_block = to_vertex_split(cotangent)
    feat_count = lax.axis_size("feat")
    bias_full = lax.all_to_all(
        jnp.broadcast_to(bias_vec[None, :], (feat_count, channels)),
        "feat",
        split_axis=0,
        concat_axis=0,
        tiled=True,
    ).reshape(-1)
    mixed_state = jnp.sum(depth_weight[:, :, None] * states, axis=0).astype(jnp.bfloat16)
    outgoing = mixed_state[:, my_send]
    incoming = lax.all_to_all(outgoing, "vert", split_axis=1, concat_axis=1, tiled=True)
    extended = jnp.concatenate([mixed_state, incoming.reshape(channels, -1)], axis=1)
    extended = extended.reshape(channels, src_blocks, block_size)
    aggregated = over_tiles(
        tile_forward, extended, my_tiles, my_dst, my_src, tile_total, row_blocks
    )
    aggregated = aggregated.reshape(channels, row_count).astype(jnp.bfloat16)
    agg_block = to_vertex_split(aggregated)
    pre_act = lax.dot_general(
        weight, agg_block, (((0,), (0,)), ((), ())), preferred_element_type=jnp.float32
    )
    pre_act = pre_act + bias_full[:, None]
    sigmoid_pre = jax.nn.sigmoid(pre_act)
    out_block = (pre_act * sigmoid_pre).astype(jnp.bfloat16)
    grad_pre = (
        cot_block.astype(jnp.float32) * sigmoid_pre * (1.0 + pre_act * (1.0 - sigmoid_pre))
    ).astype(jnp.bfloat16)
    grad_agg_block = jnp.dot(weight, grad_pre, preferred_element_type=jnp.float32).astype(
        jnp.bfloat16
    )
    weight_terms = lax.dot_general(
        agg_block, grad_pre, (((1,), (1,)), ((), ())), preferred_element_type=jnp.float32
    )
    bias_terms = jnp.sum(grad_pre.astype(jnp.float32), axis=1)
    layer_out = to_channel_split(out_block)
    grad_agg = to_channel_split(grad_agg_block)
    grad_blocks = grad_agg.reshape(channels, row_blocks, block_size)
    spread_out = over_tiles(
        tile_backward, grad_blocks, my_tiles, my_dst, my_src, tile_total, src_blocks
    )
    spread_out = spread_out.reshape(channels, src_blocks * block_size)
    halo_terms = (
        spread_out[:, row_count:].astype(jnp.bfloat16).reshape(channels, section_count, halo_width)
    )
    returned = lax.all_to_all(halo_terms, "vert", split_axis=1, concat_axis=1, tiled=True)
    grad_mixed = spread_out[:, :row_count].at[:, my_send].add(returned.astype(jnp.float32))
    grad_states = (depth_weight[:, :, None] * grad_mixed[None]).astype(jnp.bfloat16)
    depth_terms = jnp.sum(states * grad_mixed[None], axis=2)
    packed = jnp.concatenate([weight_terms, bias_terms[:, None]], axis=1)
    packed = lax.psum_scatter(packed, "feat", scatter_dimension=0, tiled=True)
    flat = jnp.concatenate([packed.reshape(-1), depth_terms.reshape(-1)])
    flat = lax.all_to_all(
        jnp.broadcast_to(flat[None, :], (vert_count, flat.shape[0])),
        "vert",
        split_axis=0,
        concat_axis=0,
        tiled=True,
    ).sum(axis=0)
    width = weight.shape[1]
    packed_sum = flat[: packed.size].reshape(packed.shape)
    depth_sum = flat[packed.size :].reshape(depth_terms.shape)
    return (
        layer_out,
        grad_states,
        packed_sum[:, :width] * norm_scale,
        packed_sum[:, width] * norm_scale,
        depth_sum * norm_scale,
    )


def solution(mesh):
    placed = (
        P(None, "feat", "vert"),
        P(None, "feat"),
        P("vert", None, None, None),
        P("vert", None),
        P("vert", None),
        P("vert"),
        P("vert", None, None),
        P(),
        P("feat"),
        P("feat", "vert"),
    )
    return jax.shard_map(
        local,
        mesh=mesh,
        in_specs=placed,
        out_specs=(
            P("feat", "vert"),
            P(None, "feat", "vert"),
            P("feat", None),
            P("feat"),
            P(None, "feat"),
        ),
        check_vma=False,
    )
```

```python
import math

import jax
import jax.numpy as jnp
from jax import lax
from jax.sharding import PartitionSpec as P


def tile_forward(extended, tile_grp, dst_grp, src_grp, live_mask, row_blocks):
    picked = jnp.take(extended, src_grp, axis=1)
    products = jnp.einsum("dtc,trc->dtr", picked, tile_grp, preferred_element_type=jnp.float32)
    onehot = (
        (dst_grp[:, None] == jnp.arange(row_blocks, dtype=jnp.int32)[None, :]) & live_mask[:, None]
    ).astype(jnp.float32)
    return jnp.einsum("dtr,tn->dnr", products, onehot)


def tile_backward(grad_blocks, tile_grp, dst_grp, src_grp, live_mask, src_blocks):
    picked = jnp.take(grad_blocks, dst_grp, axis=1)
    products = jnp.einsum("dtr,trc->dtc", picked, tile_grp, preferred_element_type=jnp.float32)
    onehot = (
        (src_grp[:, None] == jnp.arange(src_blocks, dtype=jnp.int32)[None, :]) & live_mask[:, None]
    ).astype(jnp.float32)
    return jnp.einsum("dtc,ts->dsc", products, onehot)


def over_tiles(kernel, source, tile_values, tile_dst, tile_src, tile_total, out_blocks):
    capacity = tile_values.shape[0]
    live_mask = jnp.arange(capacity, dtype=jnp.int32) < tile_total
    return kernel(source, tile_values, tile_dst, tile_src, live_mask, out_blocks)


def to_vertex_split(panel):
    return lax.all_to_all(panel, "feat", split_axis=1, concat_axis=0, tiled=True)


def to_channel_split(block):
    return lax.all_to_all(block, "feat", split_axis=0, concat_axis=1, tiled=True)


def local(
    states,
    depth_weight,
    tile_values,
    tile_dst,
    tile_src,
    tile_count,
    send_rows,
    weight,
    bias_vec,
    cotangent,
):
    channels = states.shape[1]
    row_count = states.shape[2]
    block_size = tile_values.shape[2]
    row_blocks = row_count // block_size
    my_tiles = tile_values[0]
    my_dst = tile_dst[0]
    my_src = tile_src[0]
    tile_total = tile_count[0]
    my_send = send_rows[0]
    section_count = my_send.shape[0]
    halo_width = my_send.shape[1]
    vert_count = lax.axis_size("vert")
    src_blocks = (row_count + section_count * halo_width) // block_size
    norm_scale = 1.0 / math.sqrt(vert_count * row_count)
    cot_block = to_vertex_split(cotangent)
    feat_count = lax.axis_size("feat")
    bias_full = lax.all_to_all(
        jnp.broadcast_to(bias_vec[None, :], (feat_count, channels)),
        "feat",
        split_axis=0,
        concat_axis=0,
        tiled=True,
    ).reshape(-1)
    mixed_state = jnp.sum(depth_weight[:, :, None] * states, axis=0).astype(jnp.bfloat16)
    outgoing = mixed_state[:, my_send]
    incoming = lax.all_to_all(outgoing, "vert", split_axis=1, concat_axis=1, tiled=True)
    extended = jnp.concatenate([mixed_state, incoming.reshape(channels, -1)], axis=1)
    extended = extended.reshape(channels, src_blocks, block_size)
    aggregated = over_tiles(
        tile_forward, extended, my_tiles, my_dst, my_src, tile_total, row_blocks
    )
    aggregated = aggregated.reshape(channels, row_count).astype(jnp.bfloat16)
    agg_block = to_vertex_split(aggregated)
    pre_act = lax.dot_general(
        weight, agg_block, (((0,), (0,)), ((), ())), preferred_element_type=jnp.float32
    )
    pre_act = pre_act + bias_full[:, None]
    sigmoid_pre = jax.nn.sigmoid(pre_act)
    out_block = (pre_act * sigmoid_pre).astype(jnp.bfloat16)
    grad_pre = (
        cot_block.astype(jnp.float32) * sigmoid_pre * (1.0 + pre_act * (1.0 - sigmoid_pre))
    ).astype(jnp.bfloat16)
    grad_agg_block = jnp.dot(weight, grad_pre, preferred_element_type=jnp.float32).astype(
        jnp.bfloat16
    )
    weight_terms = lax.dot_general(
        agg_block, grad_pre, (((1,), (1,)), ((), ())), preferred_element_type=jnp.float32
    )
    bias_terms = jnp.sum(grad_pre.astype(jnp.float32), axis=1)
    layer_out = to_channel_split(out_block)
    grad_agg = to_channel_split(grad_agg_block)
    grad_blocks = grad_agg.reshape(channels, row_blocks, block_size)
    spread_out = over_tiles(
        tile_backward, grad_blocks, my_tiles, my_dst, my_src, tile_total, src_blocks
    )
    spread_out = spread_out.reshape(channels, src_blocks * block_size)
    halo_terms = (
        spread_out[:, row_count:].astype(jnp.bfloat16).reshape(channels, section_count, halo_width)
    )
    returned = lax.all_to_all(halo_terms, "vert", split_axis=1, concat_axis=1, tiled=True)
    grad_mixed = spread_out[:, :row_count].at[:, my_send].add(returned.astype(jnp.float32))
    grad_states = (depth_weight[:, :, None] * grad_mixed[None]).astype(jnp.bfloat16)
    depth_terms = jnp.sum(states * grad_mixed[None], axis=2)
    packed = jnp.concatenate([weight_terms, bias_terms[:, None]], axis=1)
    packed = packed.reshape(feat_count, channels, packed.shape[1])
    packed = lax.all_to_all(packed, "feat", split_axis=0, concat_axis=0, tiled=True).sum(axis=0)
    flat = jnp.concatenate([packed.reshape(-1), depth_terms.reshape(-1)])
    flat = lax.all_to_all(
        jnp.broadcast_to(flat[None, :], (vert_count, flat.shape[0])),
        "vert",
        split_axis=0,
        concat_axis=0,
        tiled=True,
    ).sum(axis=0)
    width = weight.shape[1]
    packed_sum = flat[: packed.size].reshape(packed.shape)
    depth_sum = flat[packed.size :].reshape(depth_terms.shape)
    return (
        layer_out,
        grad_states,
        packed_sum[:, :width] * norm_scale,
        packed_sum[:, width] * norm_scale,
        depth_sum * norm_scale,
    )


def solution(mesh):
    placed = (
        P(None, "feat", "vert"),
        P(None, "feat"),
        P("vert", None, None, None),
        P("vert", None),
        P("vert", None),
        P("vert"),
        P("vert", None, None),
        P(),
        P("feat"),
        P("feat", "vert"),
    )
    return jax.shard_map(
        local,
        mesh=mesh,
        in_specs=placed,
        out_specs=(
            P("feat", "vert"),
            P(None, "feat", "vert"),
            P("feat", None),
            P("feat"),
            P(None, "feat"),
        ),
        check_vma=False,
    )
```

```python
import math

import jax
import jax.numpy as jnp
from jax import lax
from jax.sharding import PartitionSpec as P


def tile_forward(extended, tile_grp, dst_grp, src_grp, live_mask, row_blocks):
    picked = jnp.take(extended, src_grp, axis=1)
    products = jnp.einsum("dtc,trc->dtr", picked, tile_grp, preferred_element_type=jnp.float32)
    onehot = (
        (dst_grp[:, None] == jnp.arange(row_blocks, dtype=jnp.int32)[None, :]) & live_mask[:, None]
    ).astype(jnp.float32)
    return jnp.einsum("dtr,tn->dnr", products, onehot)


def tile_backward(grad_blocks, tile_grp, dst_grp, src_grp, live_mask, src_blocks):
    picked = jnp.take(grad_blocks, dst_grp, axis=1)
    products = jnp.einsum("dtr,trc->dtc", picked, tile_grp, preferred_element_type=jnp.float32)
    onehot = (
        (src_grp[:, None] == jnp.arange(src_blocks, dtype=jnp.int32)[None, :]) & live_mask[:, None]
    ).astype(jnp.float32)
    return jnp.einsum("dtc,ts->dsc", products, onehot)


def over_tiles(kernel, source, tile_values, tile_dst, tile_src, tile_total, out_blocks):
    capacity = tile_values.shape[0]
    live_mask = jnp.arange(capacity, dtype=jnp.int32) < tile_total
    return kernel(source, tile_values, tile_dst, tile_src, live_mask, out_blocks)


def local(
    states,
    depth_weight,
    tile_values,
    tile_dst,
    tile_src,
    tile_count,
    send_rows,
    weight,
    bias_vec,
    cotangent,
):
    f32 = jnp.float32
    bf16 = jnp.bfloat16
    channels = states.shape[1]
    row_count = states.shape[2]
    block_size = tile_values.shape[2]
    row_blocks = row_count // block_size
    my_tiles = tile_values[0]
    my_dst = tile_dst[0]
    my_src = tile_src[0]
    tile_total = tile_count[0]
    my_send = send_rows[0]
    section_count = my_send.shape[0]
    halo_width = my_send.shape[1]
    vert_count = lax.axis_size("vert")
    feat_count = lax.axis_size("feat")
    col_width = row_count // feat_count
    width = weight.shape[1]
    src_blocks = (row_count + section_count * halo_width) // block_size
    norm_scale = 1.0 / math.sqrt(vert_count * row_count)

    def to_blocks(x):
        return x.reshape(channels, feat_count, col_width).transpose(1, 0, 2)

    def from_blocks(x):
        return x.transpose(1, 0, 2).reshape(channels, row_count)

    halo_states = lax.all_to_all(
        states[:, :, my_send], "vert", split_axis=2, concat_axis=2, tiled=True
    )
    mixed_state = jnp.sum(depth_weight[:, :, None] * states, axis=0).astype(bf16)
    mixed_halo = jnp.sum(depth_weight[:, :, None, None] * halo_states, axis=0).astype(bf16)
    extended = jnp.concatenate([mixed_state, mixed_halo.reshape(channels, -1)], axis=1)
    extended = extended.reshape(channels, src_blocks, block_size)
    aggregated = over_tiles(
        tile_forward, extended, my_tiles, my_dst, my_src, tile_total, row_blocks
    )
    aggregated = aggregated.reshape(channels, row_count).astype(bf16)

    bias_cols = jnp.broadcast_to(bias_vec[None, :, None], (feat_count, channels, 1))
    first_send = jnp.concatenate(
        [to_blocks(aggregated).astype(f32), to_blocks(cotangent).astype(f32), bias_cols], axis=2
    )
    first_recv = lax.all_to_all(first_send, "feat", split_axis=0, concat_axis=0, tiled=True)
    first_recv = first_recv.reshape(feat_count * channels, -1)
    agg_block = first_recv[:, :col_width].astype(bf16)
    cot_block = first_recv[:, col_width : 2 * col_width]
    bias_full = first_recv[:, 2 * col_width]

    pre_act = lax.dot_general(
        weight, agg_block, (((0,), (0,)), ((), ())), preferred_element_type=f32
    )
    pre_act = pre_act + bias_full[:, None]
    sigmoid_pre = jax.nn.sigmoid(pre_act)
    out_block = (pre_act * sigmoid_pre).astype(bf16)
    grad_pre = (cot_block * sigmoid_pre * (1.0 + pre_act * (1.0 - sigmoid_pre))).astype(bf16)
    grad_agg_block = jnp.dot(weight, grad_pre, preferred_element_type=f32).astype(bf16)
    weight_terms = lax.dot_general(
        agg_block, grad_pre, (((1,), (1,)), ((), ())), preferred_element_type=f32
    )
    bias_terms = jnp.sum(grad_pre.astype(f32), axis=1)

    second_send = jnp.concatenate(
        [
            out_block.astype(f32).reshape(feat_count, channels, col_width),
            grad_agg_block.astype(f32).reshape(feat_count, channels, col_width),
            weight_terms.reshape(feat_count, channels, width),
            bias_terms.reshape(feat_count, channels, 1),
        ],
        axis=2,
    )
    second_recv = lax.all_to_all(second_send, "feat", split_axis=0, concat_axis=0, tiled=True)
    layer_out = from_blocks(second_recv[:, :, :col_width]).astype(bf16)
    grad_agg = from_blocks(second_recv[:, :, col_width : 2 * col_width]).astype(bf16)
    panel_terms = jnp.sum(second_recv[:, :, 2 * col_width :], axis=0)

    grad_blocks = grad_agg.reshape(channels, row_blocks, block_size)
    spread_out = over_tiles(
        tile_backward, grad_blocks, my_tiles, my_dst, my_src, tile_total, src_blocks
    )
    spread_out = spread_out.reshape(channels, src_blocks * block_size)
    own_grad = spread_out[:, :row_count]
    halo_terms = (
        spread_out[:, row_count:]
        .astype(bf16)
        .astype(f32)
        .reshape(channels, section_count, halo_width)
    )
    depth_terms = jnp.sum(states * own_grad[None], axis=2) + jnp.sum(
        halo_states * halo_terms[None], axis=(2, 3)
    )
    totals = jnp.concatenate([panel_terms.reshape(-1), depth_terms.reshape(-1)])
    last_send = jnp.concatenate(
        [
            halo_terms.transpose(1, 0, 2).reshape(section_count, channels * halo_width),
            jnp.broadcast_to(totals[None, :], (vert_count, totals.shape[0])),
        ],
        axis=1,
    )
    last_recv = lax.all_to_all(last_send, "vert", split_axis=0, concat_axis=0, tiled=True)
    returned = (
        last_recv[:, : channels * halo_width]
        .reshape(section_count, channels, halo_width)
        .transpose(1, 0, 2)
    )
    totals = jnp.sum(last_recv[:, channels * halo_width :], axis=0)
    grad_mixed = own_grad.at[:, my_send].add(returned)
    grad_states = (depth_weight[:, :, None] * grad_mixed[None]).astype(bf16)
    panel_sum = totals[: panel_terms.size].reshape(panel_terms.shape)
    depth_sum = totals[panel_terms.size :].reshape(depth_terms.shape)
    return (
        layer_out,
        grad_states,
        panel_sum[:, :width] * norm_scale,
        panel_sum[:, width] * norm_scale,
        depth_sum * norm_scale,
    )


def solution(mesh):
    placed = (
        P(None, "feat", "vert"),
        P(None, "feat"),
        P("vert", None, None, None),
        P("vert", None),
        P("vert", None),
        P("vert"),
        P("vert", None, None),
        P(),
        P("feat"),
        P("feat", "vert"),
    )
    return jax.shard_map(
        local,
        mesh=mesh,
        in_specs=placed,
        out_specs=(
            P("feat", "vert"),
            P(None, "feat", "vert"),
            P("feat", None),
            P("feat"),
            P(None, "feat"),
        ),
        check_vma=False,
    )
```

```python
import math

import jax
import jax.numpy as jnp
from jax import lax
from jax.sharding import PartitionSpec as P


def tile_forward(extended, tile_grp, dst_grp, src_grp, live_mask, row_blocks):
    picked = jnp.take(extended, src_grp, axis=1)
    products = jnp.einsum("dtc,trc->dtr", picked, tile_grp, preferred_element_type=jnp.float32)
    onehot = (
        (dst_grp[:, None] == jnp.arange(row_blocks, dtype=jnp.int32)[None, :]) & live_mask[:, None]
    ).astype(jnp.float32)
    return jnp.einsum("dtr,tn->dnr", products, onehot)


def tile_backward(grad_blocks, tile_grp, dst_grp, src_grp, live_mask, src_blocks):
    picked = jnp.take(grad_blocks, dst_grp, axis=1)
    products = jnp.einsum("dtr,trc->dtc", picked, tile_grp, preferred_element_type=jnp.float32)
    onehot = (
        (src_grp[:, None] == jnp.arange(src_blocks, dtype=jnp.int32)[None, :]) & live_mask[:, None]
    ).astype(jnp.float32)
    return jnp.einsum("dtc,ts->dsc", products, onehot)


def over_tiles(kernel, source, tile_values, tile_dst, tile_src, tile_total, out_blocks):
    capacity = tile_values.shape[0]
    live_mask = jnp.arange(capacity, dtype=jnp.int32) < tile_total
    return kernel(source, tile_values, tile_dst, tile_src, live_mask, out_blocks)


def local(
    states,
    depth_weight,
    tile_values,
    tile_dst,
    tile_src,
    tile_count,
    send_rows,
    weight,
    bias_vec,
    cotangent,
):
    f32 = jnp.float32
    bf16 = jnp.bfloat16
    channels = states.shape[1]
    row_count = states.shape[2]
    block_size = tile_values.shape[2]
    row_blocks = row_count // block_size
    my_tiles = tile_values[0]
    my_dst = tile_dst[0]
    my_src = tile_src[0]
    tile_total = tile_count[0]
    my_send = send_rows[0]
    section_count = my_send.shape[0]
    halo_width = my_send.shape[1]
    vert_count = lax.axis_size("vert")
    feat_count = lax.axis_size("feat")
    col_width = row_count // feat_count
    width = weight.shape[1]
    src_blocks = (row_count + section_count * halo_width) // block_size
    norm_scale = 1.0 / math.sqrt(vert_count * row_count)

    def to_blocks(x):
        return x.reshape(channels, feat_count, col_width).transpose(1, 0, 2)

    def from_blocks(x):
        return x.transpose(1, 0, 2).reshape(channels, row_count)

    state_count = states.shape[0]
    listed = jnp.take(states.reshape(state_count * channels, row_count), my_send.reshape(-1), axis=1)
    halo_states = lax.all_to_all(
        listed.reshape(state_count, channels, section_count, halo_width),
        "vert",
        split_axis=2,
        concat_axis=2,
        tiled=True,
    )
    mixed_state = jnp.sum(depth_weight[:, :, None] * states, axis=0).astype(bf16)
    mixed_halo = jnp.sum(depth_weight[:, :, None, None] * halo_states, axis=0).astype(bf16)
    extended = jnp.concatenate([mixed_state, mixed_halo.reshape(channels, -1)], axis=1)
    extended = extended.reshape(channels, src_blocks, block_size)
    aggregated = over_tiles(
        tile_forward, extended, my_tiles, my_dst, my_src, tile_total, row_blocks
    )
    aggregated = aggregated.reshape(channels, row_count).astype(bf16)

    bias_cols = jnp.broadcast_to(bias_vec[None, :, None], (feat_count, channels, 1))
    first_send = jnp.concatenate(
        [to_blocks(aggregated).astype(f32), to_blocks(cotangent).astype(f32), bias_cols], axis=2
    )
    first_recv = lax.all_to_all(first_send, "feat", split_axis=0, concat_axis=0, tiled=True)
    first_recv = first_recv.reshape(feat_count * channels, -1)
    agg_block = first_recv[:, :col_width].astype(bf16)
    cot_block = first_recv[:, col_width : 2 * col_width]
    bias_full = first_recv[:, 2 * col_width]

    pre_act = lax.dot_general(
        weight, agg_block, (((0,), (0,)), ((), ())), preferred_element_type=f32
    )
    pre_act = pre_act + bias_full[:, None]
    sigmoid_pre = jax.nn.sigmoid(pre_act)
    out_block = (pre_act * sigmoid_pre).astype(bf16)
    grad_pre = (cot_block * sigmoid_pre * (1.0 + pre_act * (1.0 - sigmoid_pre))).astype(bf16)
    grad_agg_block = jnp.dot(weight, grad_pre, preferred_element_type=f32).astype(bf16)
    weight_terms = lax.dot_general(
        agg_block, grad_pre, (((1,), (1,)), ((), ())), preferred_element_type=f32
    )
    bias_terms = jnp.sum(grad_pre.astype(f32), axis=1)

    second_send = jnp.concatenate(
        [
            out_block.astype(f32).reshape(feat_count, channels, col_width),
            grad_agg_block.astype(f32).reshape(feat_count, channels, col_width),
            weight_terms.reshape(feat_count, channels, width),
            bias_terms.reshape(feat_count, channels, 1),
        ],
        axis=2,
    )
    second_recv = lax.all_to_all(second_send, "feat", split_axis=0, concat_axis=0, tiled=True)
    layer_out = from_blocks(second_recv[:, :, :col_width]).astype(bf16)
    grad_agg = from_blocks(second_recv[:, :, col_width : 2 * col_width]).astype(bf16)
    panel_terms = jnp.sum(second_recv[:, :, 2 * col_width :], axis=0)

    grad_blocks = grad_agg.reshape(channels, row_blocks, block_size)
    spread_out = over_tiles(
        tile_backward, grad_blocks, my_tiles, my_dst, my_src, tile_total, src_blocks
    )
    spread_out = spread_out.reshape(channels, src_blocks * block_size)
    own_grad = spread_out[:, :row_count]
    halo_terms = (
        spread_out[:, row_count:]
        .astype(bf16)
        .astype(f32)
        .reshape(channels, section_count, halo_width)
    )
    depth_terms = jnp.sum(states * own_grad[None], axis=2) + jnp.sum(
        halo_states * halo_terms[None], axis=(2, 3)
    )
    totals = jnp.concatenate([panel_terms.reshape(-1), depth_terms.reshape(-1)])
    last_send = jnp.concatenate(
        [
            halo_terms.transpose(1, 0, 2).reshape(section_count, channels * halo_width),
            jnp.broadcast_to(totals[None, :], (vert_count, totals.shape[0])),
        ],
        axis=1,
    )
    last_recv = lax.all_to_all(last_send, "vert", split_axis=0, concat_axis=0, tiled=True)
    returned = (
        last_recv[:, : channels * halo_width]
        .reshape(section_count, channels, halo_width)
        .transpose(1, 0, 2)
    )
    totals = jnp.sum(last_recv[:, channels * halo_width :], axis=0)
    grad_mixed = own_grad.at[:, my_send].add(returned)
    grad_states = (depth_weight[:, :, None] * grad_mixed[None]).astype(bf16)
    panel_sum = totals[: panel_terms.size].reshape(panel_terms.shape)
    depth_sum = totals[panel_terms.size :].reshape(depth_terms.shape)
    return (
        layer_out,
        grad_states,
        panel_sum[:, :width] * norm_scale,
        panel_sum[:, width] * norm_scale,
        depth_sum * norm_scale,
    )


def solution(mesh):
    placed = (
        P(None, "feat", "vert"),
        P(None, "feat"),
        P("vert", None, None, None),
        P("vert", None),
        P("vert", None),
        P("vert"),
        P("vert", None, None),
        P(),
        P("feat"),
        P("feat", "vert"),
    )
    return jax.shard_map(
        local,
        mesh=mesh,
        in_specs=placed,
        out_specs=(
            P("feat", "vert"),
            P(None, "feat", "vert"),
            P("feat", None),
            P("feat"),
            P(None, "feat"),
        ),
        check_vma=False,
    )
```

```python
import math

import jax
import jax.numpy as jnp
from jax import lax
from jax.sharding import PartitionSpec as P


def tile_forward(extended, tile_grp, dst_grp, src_grp, live_mask, row_blocks):
    picked = jnp.take(extended, src_grp, axis=1)
    products = jnp.einsum("dtc,trc->dtr", picked, tile_grp, preferred_element_type=jnp.float32)
    onehot = (
        (dst_grp[:, None] == jnp.arange(row_blocks, dtype=jnp.int32)[None, :]) & live_mask[:, None]
    ).astype(jnp.float32)
    return jnp.einsum("dtr,tn->dnr", products, onehot)


def tile_backward(grad_blocks, tile_grp, dst_grp, src_grp, live_mask, src_blocks):
    picked = jnp.take(grad_blocks, dst_grp, axis=1)
    products = jnp.einsum("dtr,trc->dtc", picked, tile_grp, preferred_element_type=jnp.float32)
    onehot = (
        (src_grp[:, None] == jnp.arange(src_blocks, dtype=jnp.int32)[None, :]) & live_mask[:, None]
    ).astype(jnp.float32)
    return jnp.einsum("dtc,ts->dsc", products, onehot)


def over_tiles(kernel, source, tile_values, tile_dst, tile_src, tile_total, out_blocks):
    capacity = tile_values.shape[0]
    live_mask = jnp.arange(capacity, dtype=jnp.int32) < tile_total
    return kernel(source, tile_values, tile_dst, tile_src, live_mask, out_blocks)


def local(
    states,
    depth_weight,
    tile_values,
    tile_dst,
    tile_src,
    tile_count,
    send_rows,
    weight,
    bias_vec,
    cotangent,
):
    f32 = jnp.float32
    bf16 = jnp.bfloat16
    channels = states.shape[1]
    row_count = states.shape[2]
    block_size = tile_values.shape[2]
    row_blocks = row_count // block_size
    my_tiles = tile_values[0]
    my_dst = tile_dst[0]
    my_src = tile_src[0]
    tile_total = tile_count[0]
    my_send = send_rows[0]
    section_count = my_send.shape[0]
    halo_width = my_send.shape[1]
    vert_count = lax.axis_size("vert")
    feat_count = lax.axis_size("feat")
    col_width = row_count // feat_count
    width = weight.shape[1]
    src_blocks = (row_count + section_count * halo_width) // block_size
    norm_scale = 1.0 / math.sqrt(vert_count * row_count)

    def to_blocks(x):
        return x.reshape(channels, feat_count, col_width).transpose(1, 0, 2)

    def from_blocks(x):
        return x.transpose(1, 0, 2).reshape(channels, row_count)

    state_count = states.shape[0]
    listed = jnp.take(states.reshape(state_count * channels, row_count), my_send.reshape(-1), axis=1)
    halo_states = lax.all_to_all(
        listed.reshape(state_count, channels, section_count, halo_width),
        "vert",
        split_axis=2,
        concat_axis=2,
        tiled=True,
    )
    mixed_state = jnp.sum(depth_weight[:, :, None] * states, axis=0).astype(bf16)
    mixed_halo = jnp.sum(depth_weight[:, :, None, None] * halo_states, axis=0).astype(bf16)
    extended = jnp.concatenate([mixed_state, mixed_halo.reshape(channels, -1)], axis=1)
    extended = extended.reshape(channels, src_blocks, block_size)
    aggregated = over_tiles(
        tile_forward, extended, my_tiles, my_dst, my_src, tile_total, row_blocks
    )
    aggregated = aggregated.reshape(channels, row_count).astype(bf16)

    bias_cols = jnp.broadcast_to(bias_vec[None, :, None], (feat_count, channels, 1))
    first_send = jnp.concatenate(
        [to_blocks(aggregated).astype(f32), to_blocks(cotangent).astype(f32), bias_cols], axis=2
    )
    first_recv = lax.all_to_all(first_send, "feat", split_axis=0, concat_axis=0, tiled=True)
    first_recv = first_recv.reshape(feat_count * channels, -1)
    agg_block = first_recv[:, :col_width].astype(bf16)
    cot_block = first_recv[:, col_width : 2 * col_width]
    bias_full = first_recv[:, 2 * col_width]

    pre_act = lax.dot_general(
        weight, agg_block, (((0,), (0,)), ((), ())), preferred_element_type=f32
    )
    pre_act = pre_act + bias_full[:, None]
    sigmoid_pre = jax.nn.sigmoid(pre_act)
    out_block = (pre_act * sigmoid_pre).astype(bf16)
    grad_pre = (cot_block * sigmoid_pre * (1.0 + pre_act * (1.0 - sigmoid_pre))).astype(bf16)
    grad_agg_block = jnp.dot(weight, grad_pre, preferred_element_type=f32).astype(bf16)
    weight_terms = lax.dot_general(
        agg_block, grad_pre, (((1,), (1,)), ((), ())), preferred_element_type=f32
    )
    bias_terms = jnp.sum(grad_pre.astype(f32), axis=1)

    second_send = jnp.concatenate(
        [
            out_block.astype(f32).reshape(feat_count, channels, col_width),
            grad_agg_block.astype(f32).reshape(feat_count, channels, col_width),
            weight_terms.reshape(feat_count, channels, width),
            bias_terms.reshape(feat_count, channels, 1),
        ],
        axis=2,
    )
    second_recv = lax.all_to_all(second_send, "feat", split_axis=0, concat_axis=0, tiled=True)
    layer_out = from_blocks(second_recv[:, :, :col_width]).astype(bf16)
    grad_agg = from_blocks(second_recv[:, :, col_width : 2 * col_width]).astype(bf16)
    panel_terms = jnp.sum(second_recv[:, :, 2 * col_width :], axis=0)

    grad_blocks = grad_agg.reshape(channels, row_blocks, block_size)
    spread_out = over_tiles(
        tile_backward, grad_blocks, my_tiles, my_dst, my_src, tile_total, src_blocks
    )
    spread_out = spread_out.reshape(channels, src_blocks * block_size)
    own_grad = spread_out[:, :row_count]
    halo_terms = (
        spread_out[:, row_count:]
        .astype(bf16)
        .astype(f32)
        .reshape(channels, section_count, halo_width)
    )
    depth_terms = jnp.sum(states * own_grad[None], axis=2) + jnp.sum(
        halo_states * halo_terms[None], axis=(2, 3)
    )
    totals = jnp.concatenate([panel_terms.reshape(-1), depth_terms.reshape(-1)])
    last_send = jnp.concatenate(
        [
            halo_terms.transpose(1, 0, 2).reshape(section_count, channels * halo_width),
            jnp.broadcast_to(totals[None, :], (vert_count, totals.shape[0])),
        ],
        axis=1,
    )
    last_recv = lax.all_to_all(last_send, "vert", split_axis=0, concat_axis=0, tiled=True)
    returned = (
        last_recv[:, : channels * halo_width]
        .reshape(section_count, channels, halo_width)
        .transpose(1, 0, 2)
    )
    totals = jnp.sum(last_recv[:, channels * halo_width :], axis=0)
    hot = (
        my_send.reshape(-1)[None, :] == jnp.arange(row_count, dtype=jnp.int32)[:, None]
    ).astype(bf16)
    added = lax.dot_general(
        hot,
        returned.reshape(channels, -1).astype(bf16),
        (((1,), (1,)), ((), ())),
        preferred_element_type=f32,
    )
    grad_mixed = own_grad + added.T
    grad_states = (depth_weight[:, :, None] * grad_mixed[None]).astype(bf16)
    panel_sum = totals[: panel_terms.size].reshape(panel_terms.shape)
    depth_sum = totals[panel_terms.size :].reshape(depth_terms.shape)
    return (
        layer_out,
        grad_states,
        panel_sum[:, :width] * norm_scale,
        panel_sum[:, width] * norm_scale,
        depth_sum * norm_scale,
    )


def solution(mesh):
    placed = (
        P(None, "feat", "vert"),
        P(None, "feat"),
        P("vert", None, None, None),
        P("vert", None),
        P("vert", None),
        P("vert"),
        P("vert", None, None),
        P(),
        P("feat"),
        P("feat", "vert"),
    )
    return jax.shard_map(
        local,
        mesh=mesh,
        in_specs=placed,
        out_specs=(
            P("feat", "vert"),
            P(None, "feat", "vert"),
            P("feat", None),
            P("feat"),
            P(None, "feat"),
        ),
        check_vma=False,
    )
```

```python
import math

import jax
import jax.numpy as jnp
from jax import lax
from jax.sharding import PartitionSpec as P


def tile_forward(extended, tile_grp, dst_grp, src_grp, live_mask, row_blocks):
    picked = jnp.take(extended, src_grp, axis=1)
    products = jnp.einsum("dtc,trc->dtr", picked, tile_grp, preferred_element_type=jnp.float32)
    onehot = (
        (dst_grp[:, None] == jnp.arange(row_blocks, dtype=jnp.int32)[None, :]) & live_mask[:, None]
    ).astype(jnp.float32)
    return jnp.einsum("dtr,tn->dnr", products, onehot)


def tile_backward(grad_blocks, tile_grp, dst_grp, src_grp, live_mask, src_blocks):
    picked = jnp.take(grad_blocks, dst_grp, axis=1)
    products = jnp.einsum("dtr,trc->dtc", picked, tile_grp, preferred_element_type=jnp.float32)
    onehot = (
        (src_grp[:, None] == jnp.arange(src_blocks, dtype=jnp.int32)[None, :]) & live_mask[:, None]
    ).astype(jnp.float32)
    return jnp.einsum("dtc,ts->dsc", products, onehot)


def over_tiles(kernel, source, tile_values, tile_dst, tile_src, tile_total, out_blocks):
    capacity = tile_values.shape[0]
    live_mask = jnp.arange(capacity, dtype=jnp.int32) < tile_total
    return kernel(source, tile_values, tile_dst, tile_src, live_mask, out_blocks)


def bf16_parts(x, count):
    parts = []
    rest = x
    for _ in range(count - 1):
        head = lax.reduce_precision(rest, exponent_bits=8, mantissa_bits=7)
        parts.append(head.astype(jnp.bfloat16))
        rest = rest - head
    parts.append(rest.astype(jnp.bfloat16))
    return parts


def parts_sum(parts):
    total = parts[0].astype(jnp.float32)
    for part in parts[1:]:
        total = total + part.astype(jnp.float32)
    return total


def local(
    states,
    depth_weight,
    tile_values,
    tile_dst,
    tile_src,
    tile_count,
    send_rows,
    weight,
    bias_vec,
    cotangent,
):
    f32 = jnp.float32
    bf16 = jnp.bfloat16
    channels = states.shape[1]
    row_count = states.shape[2]
    block_size = tile_values.shape[2]
    row_blocks = row_count // block_size
    my_tiles = tile_values[0]
    my_dst = tile_dst[0]
    my_src = tile_src[0]
    tile_total = tile_count[0]
    my_send = send_rows[0]
    section_count = my_send.shape[0]
    halo_width = my_send.shape[1]
    vert_count = lax.axis_size("vert")
    feat_count = lax.axis_size("feat")
    col_width = row_count // feat_count
    width = weight.shape[1]
    src_blocks = (row_count + section_count * halo_width) // block_size
    norm_scale = 1.0 / math.sqrt(vert_count * row_count)

    def to_blocks(x):
        return x.reshape(channels, feat_count, col_width).transpose(1, 0, 2)

    def from_blocks(x):
        return x.transpose(1, 0, 2).reshape(channels, row_count)

    state_count = states.shape[0]
    listed = jnp.take(states.reshape(state_count * channels, row_count), my_send.reshape(-1), axis=1)
    halo_states = lax.all_to_all(
        listed.reshape(state_count, channels, section_count, halo_width),
        "vert",
        split_axis=2,
        concat_axis=2,
        tiled=True,
    )
    mixed_state = jnp.sum(depth_weight[:, :, None] * states, axis=0).astype(bf16)
    mixed_halo = jnp.sum(depth_weight[:, :, None, None] * halo_states, axis=0).astype(bf16)
    extended = jnp.concatenate([mixed_state, mixed_halo.reshape(channels, -1)], axis=1)
    extended = extended.reshape(channels, src_blocks, block_size)
    aggregated = over_tiles(
        tile_forward, extended, my_tiles, my_dst, my_src, tile_total, row_blocks
    )
    aggregated = aggregated.reshape(channels, row_count).astype(bf16)

    bias_cols = jnp.broadcast_to(
        jnp.stack(bf16_parts(bias_vec, 3), axis=1)[None], (feat_count, channels, 3)
    )
    first_send = jnp.concatenate([to_blocks(aggregated), to_blocks(cotangent), bias_cols], axis=2)
    first_recv = lax.all_to_all(first_send, "feat", split_axis=0, concat_axis=0, tiled=True)
    first_recv = first_recv.reshape(feat_count * channels, -1)
    agg_block = first_recv[:, :col_width]
    cot_block = first_recv[:, col_width : 2 * col_width].astype(f32)
    bias_full = parts_sum([first_recv[:, 2 * col_width + n] for n in range(3)])

    pre_act = lax.dot_general(
        weight, agg_block, (((0,), (0,)), ((), ())), preferred_element_type=f32
    )
    pre_act = pre_act + bias_full[:, None]
    sigmoid_pre = jax.nn.sigmoid(pre_act)
    out_block = (pre_act * sigmoid_pre).astype(bf16)
    grad_pre = (cot_block * sigmoid_pre * (1.0 + pre_act * (1.0 - sigmoid_pre))).astype(bf16)
    grad_agg_block = jnp.dot(weight, grad_pre, preferred_element_type=f32).astype(bf16)
    weight_terms = lax.dot_general(
        agg_block, grad_pre, (((1,), (1,)), ((), ())), preferred_element_type=f32
    )
    bias_terms = jnp.sum(grad_pre.astype(f32), axis=1)

    grad_terms = jnp.concatenate(
        [
            weight_terms.reshape(feat_count, channels, width),
            bias_terms.reshape(feat_count, channels, 1),
        ],
        axis=2,
    )
    second_send = jnp.concatenate(
        [
            out_block.reshape(feat_count, channels, col_width),
            grad_agg_block.reshape(feat_count, channels, col_width),
        ]
        + bf16_parts(grad_terms, 2),
        axis=2,
    )
    second_recv = lax.all_to_all(second_send, "feat", split_axis=0, concat_axis=0, tiled=True)
    layer_out = from_blocks(second_recv[:, :, :col_width])
    grad_agg = from_blocks(second_recv[:, :, col_width : 2 * col_width])
    terms_width = width + 1
    start = 2 * col_width
    panel_terms = jnp.sum(
        parts_sum(
            [
                second_recv[:, :, start : start + terms_width],
                second_recv[:, :, start + terms_width :],
            ]
        ),
        axis=0,
    )

    grad_blocks = grad_agg.reshape(channels, row_blocks, block_size)
    spread_out = over_tiles(
        tile_backward, grad_blocks, my_tiles, my_dst, my_src, tile_total, src_blocks
    )
    spread_out = spread_out.reshape(channels, src_blocks * block_size)
    own_grad = spread_out[:, :row_count]
    halo_part = spread_out[:, row_count:].reshape(channels, section_count, halo_width)
    halo_terms = lax.reduce_precision(halo_part, exponent_bits=8, mantissa_bits=7)
    depth_terms = jnp.sum(states * own_grad[None], axis=2) + jnp.sum(
        halo_states * halo_terms[None], axis=(2, 3)
    )
    totals = jnp.concatenate([panel_terms.reshape(-1), depth_terms.reshape(-1)])
    last_send = jnp.concatenate(
        [halo_part.astype(bf16).transpose(1, 0, 2).reshape(section_count, channels * halo_width)]
        + [
            jnp.broadcast_to(part[None, :], (vert_count, totals.shape[0]))
            for part in bf16_parts(totals, 2)
        ],
        axis=1,
    )
    last_recv = lax.all_to_all(last_send, "vert", split_axis=0, concat_axis=0, tiled=True)
    returned = (
        last_recv[:, : channels * halo_width]
        .reshape(section_count, channels, halo_width)
        .transpose(1, 0, 2)
    )
    tail = last_recv[:, channels * halo_width :]
    totals = jnp.sum(
        parts_sum([tail[:, : totals.shape[0]], tail[:, totals.shape[0] :]]), axis=0
    )
    hot = (
        my_send.reshape(-1)[None, :] == jnp.arange(row_count, dtype=jnp.int32)[:, None]
    ).astype(bf16)
    added = lax.dot_general(
        hot,
        returned.reshape(channels, -1),
        (((1,), (1,)), ((), ())),
        preferred_element_type=f32,
    )
    grad_mixed = own_grad + added.T
    grad_states = (depth_weight[:, :, None] * grad_mixed[None]).astype(bf16)
    panel_sum = totals[: panel_terms.size].reshape(panel_terms.shape)
    depth_sum = totals[panel_terms.size :].reshape(depth_terms.shape)
    return (
        layer_out,
        grad_states,
        panel_sum[:, :width] * norm_scale,
        panel_sum[:, width] * norm_scale,
        depth_sum * norm_scale,
    )


def solution(mesh):
    placed = (
        P(None, "feat", "vert"),
        P(None, "feat"),
        P("vert", None, None, None),
        P("vert", None),
        P("vert", None),
        P("vert"),
        P("vert", None, None),
        P(),
        P("feat"),
        P("feat", "vert"),
    )
    return jax.shard_map(
        local,
        mesh=mesh,
        in_specs=placed,
        out_specs=(
            P("feat", "vert"),
            P(None, "feat", "vert"),
            P("feat", None),
            P("feat"),
            P(None, "feat"),
        ),
        check_vma=False,
    )
```

```python
import math

import jax
import jax.numpy as jnp
from jax import lax
from jax.sharding import PartitionSpec as P


def tile_forward(extended, tile_grp, dst_grp, src_grp, live_mask, row_blocks):
    picked = extended.at[:, src_grp].get(mode="promise_in_bounds")
    products = jnp.einsum("dtc,trc->dtr", picked, tile_grp, preferred_element_type=jnp.float32)
    onehot = (
        (dst_grp[:, None] == jnp.arange(row_blocks, dtype=jnp.int32)[None, :]) & live_mask[:, None]
    ).astype(jnp.float32)
    return jnp.einsum("dtr,tn->dnr", products, onehot)


def tile_backward(grad_blocks, tile_grp, dst_grp, src_grp, live_mask, src_blocks):
    picked = grad_blocks.at[:, dst_grp].get(mode="promise_in_bounds")
    products = jnp.einsum("dtr,trc->dtc", picked, tile_grp, preferred_element_type=jnp.float32)
    onehot = (
        (src_grp[:, None] == jnp.arange(src_blocks, dtype=jnp.int32)[None, :]) & live_mask[:, None]
    ).astype(jnp.float32)
    return jnp.einsum("dtc,ts->dsc", products, onehot)


def over_tiles(kernel, source, tile_values, tile_dst, tile_src, tile_total, out_blocks):
    capacity = tile_values.shape[0]
    live_mask = jnp.arange(capacity, dtype=jnp.int32) < tile_total
    return kernel(source, tile_values, tile_dst, tile_src, live_mask, out_blocks)


def bf16_parts(x, count):
    parts = []
    rest = x
    for _ in range(count - 1):
        head = lax.reduce_precision(rest, exponent_bits=8, mantissa_bits=7)
        parts.append(head.astype(jnp.bfloat16))
        rest = rest - head
    parts.append(rest.astype(jnp.bfloat16))
    return parts


def parts_sum(parts):
    total = parts[0].astype(jnp.float32)
    for part in parts[1:]:
        total = total + part.astype(jnp.float32)
    return total


def local(
    states,
    depth_weight,
    tile_values,
    tile_dst,
    tile_src,
    tile_count,
    send_rows,
    weight,
    bias_vec,
    cotangent,
):
    f32 = jnp.float32
    bf16 = jnp.bfloat16
    channels = states.shape[1]
    row_count = states.shape[2]
    block_size = tile_values.shape[2]
    row_blocks = row_count // block_size
    my_tiles = tile_values[0]
    my_dst = tile_dst[0]
    my_src = tile_src[0]
    tile_total = tile_count[0]
    my_send = send_rows[0]
    section_count = my_send.shape[0]
    halo_width = my_send.shape[1]
    vert_count = lax.axis_size("vert")
    feat_count = lax.axis_size("feat")
    col_width = row_count // feat_count
    width = weight.shape[1]
    src_blocks = (row_count + section_count * halo_width) // block_size
    norm_scale = 1.0 / math.sqrt(vert_count * row_count)

    def to_blocks(x):
        return x.reshape(channels, feat_count, col_width).transpose(1, 0, 2)

    def from_blocks(x):
        return x.transpose(1, 0, 2).reshape(channels, row_count)

    state_count = states.shape[0]
    listed = (
        states.reshape(state_count * channels, row_count)
        .at[:, my_send.reshape(-1)]
        .get(mode="promise_in_bounds")
    )
    halo_states = lax.all_to_all(
        listed.reshape(state_count, channels, section_count, halo_width),
        "vert",
        split_axis=2,
        concat_axis=2,
        tiled=True,
    )
    mixed_state = jnp.sum(depth_weight[:, :, None] * states, axis=0).astype(bf16)
    mixed_halo = jnp.sum(depth_weight[:, :, None, None] * halo_states, axis=0).astype(bf16)
    extended = jnp.concatenate([mixed_state, mixed_halo.reshape(channels, -1)], axis=1)
    extended = extended.reshape(channels, src_blocks, block_size)
    aggregated = over_tiles(
        tile_forward, extended, my_tiles, my_dst, my_src, tile_total, row_blocks
    )
    aggregated = aggregated.reshape(channels, row_count).astype(bf16)

    bias_cols = jnp.broadcast_to(
        jnp.stack(bf16_parts(bias_vec, 3), axis=1)[None], (feat_count, channels, 3)
    )
    first_send = jnp.concatenate([to_blocks(aggregated), to_blocks(cotangent), bias_cols], axis=2)
    first_recv = lax.all_to_all(first_send, "feat", split_axis=0, concat_axis=0, tiled=True)
    first_recv = first_recv.reshape(feat_count * channels, -1)
    agg_block = first_recv[:, :col_width]
    cot_block = first_recv[:, col_width : 2 * col_width].astype(f32)
    bias_full = parts_sum([first_recv[:, 2 * col_width + n] for n in range(3)])

    pre_act = lax.dot_general(
        weight, agg_block, (((0,), (0,)), ((), ())), preferred_element_type=f32
    )
    pre_act = pre_act + bias_full[:, None]
    sigmoid_pre = jax.nn.sigmoid(pre_act)
    out_block = (pre_act * sigmoid_pre).astype(bf16)
    grad_pre = (cot_block * sigmoid_pre * (1.0 + pre_act * (1.0 - sigmoid_pre))).astype(bf16)
    grad_agg_block = jnp.dot(weight, grad_pre, preferred_element_type=f32).astype(bf16)
    weight_terms = lax.dot_general(
        agg_block, grad_pre, (((1,), (1,)), ((), ())), preferred_element_type=f32
    )
    bias_terms = jnp.sum(grad_pre.astype(f32), axis=1)

    grad_terms = jnp.concatenate(
        [
            weight_terms.reshape(feat_count, channels, width),
            bias_terms.reshape(feat_count, channels, 1),
        ],
        axis=2,
    )
    second_send = jnp.concatenate(
        [
            out_block.reshape(feat_count, channels, col_width),
            grad_agg_block.reshape(feat_count, channels, col_width),
        ]
        + bf16_parts(grad_terms, 2),
        axis=2,
    )
    second_recv = lax.all_to_all(second_send, "feat", split_axis=0, concat_axis=0, tiled=True)
    layer_out = from_blocks(second_recv[:, :, :col_width])
    grad_agg = from_blocks(second_recv[:, :, col_width : 2 * col_width])
    terms_width = width + 1
    start = 2 * col_width
    panel_terms = jnp.sum(
        parts_sum(
            [
                second_recv[:, :, start : start + terms_width],
                second_recv[:, :, start + terms_width :],
            ]
        ),
        axis=0,
    )

    grad_blocks = grad_agg.reshape(channels, row_blocks, block_size)
    spread_out = over_tiles(
        tile_backward, grad_blocks, my_tiles, my_dst, my_src, tile_total, src_blocks
    )
    spread_out = spread_out.reshape(channels, src_blocks * block_size)
    own_grad = spread_out[:, :row_count]
    halo_part = spread_out[:, row_count:].reshape(channels, section_count, halo_width)
    halo_terms = lax.reduce_precision(halo_part, exponent_bits=8, mantissa_bits=7)
    depth_terms = jnp.sum(states * own_grad[None], axis=2) + jnp.sum(
        halo_states * halo_terms[None], axis=(2, 3)
    )
    totals = jnp.concatenate([panel_terms.reshape(-1), depth_terms.reshape(-1)]) * norm_scale
    last_send = jnp.concatenate(
        [halo_part.astype(bf16).transpose(1, 0, 2).reshape(section_count, channels * halo_width)]
        + [
            jnp.broadcast_to(part[None, :], (vert_count, totals.shape[0]))
            for part in bf16_parts(totals, 2)
        ],
        axis=1,
    )
    last_recv = lax.all_to_all(last_send, "vert", split_axis=0, concat_axis=0, tiled=True)
    returned = (
        last_recv[:, : channels * halo_width]
        .reshape(section_count, channels, halo_width)
        .transpose(1, 0, 2)
    )
    tail = last_recv[:, channels * halo_width :]
    totals = jnp.sum(
        parts_sum([tail[:, : totals.shape[0]], tail[:, totals.shape[0] :]]), axis=0
    )
    hot = (
        my_send.reshape(-1)[None, :] == jnp.arange(row_count, dtype=jnp.int32)[:, None]
    ).astype(bf16)
    added = lax.dot_general(
        hot,
        returned.reshape(channels, -1),
        (((1,), (1,)), ((), ())),
        preferred_element_type=f32,
    )
    grad_mixed = own_grad + added.T
    grad_states = (depth_weight[:, :, None] * grad_mixed[None]).astype(bf16)
    panel_sum = totals[: panel_terms.size].reshape(panel_terms.shape)
    depth_sum = totals[panel_terms.size :].reshape(depth_terms.shape)
    return (
        layer_out,
        grad_states,
        panel_sum[:, :width],
        panel_sum[:, width],
        depth_sum,
    )


def solution(mesh):
    placed = (
        P(None, "feat", "vert"),
        P(None, "feat"),
        P("vert", None, None, None),
        P("vert", None),
        P("vert", None),
        P("vert"),
        P("vert", None, None),
        P(),
        P("feat"),
        P("feat", "vert"),
    )
    return jax.shard_map(
        local,
        mesh=mesh,
        in_specs=placed,
        out_specs=(
            P("feat", "vert"),
            P(None, "feat", "vert"),
            P("feat", None),
            P("feat"),
            P(None, "feat"),
        ),
        check_vma=False,
    )
```

```python
import math

import jax
import jax.numpy as jnp
from jax import lax
from jax.sharding import PartitionSpec as P


def tile_forward(extended, tile_grp, dst_grp, src_grp, live_mask, row_blocks):
    picked = extended.at[:, src_grp].get(mode="promise_in_bounds")
    products = jnp.einsum("dtc,trc->dtr", picked, tile_grp, preferred_element_type=jnp.float32)
    onehot = (
        (dst_grp[:, None] == jnp.arange(row_blocks, dtype=jnp.int32)[None, :]) & live_mask[:, None]
    ).astype(jnp.float32)
    return jnp.einsum("dtr,tn->dnr", products, onehot)


def tile_backward(grad_blocks, tile_grp, dst_grp, src_grp, live_mask, src_blocks):
    picked = grad_blocks.at[:, dst_grp].get(mode="promise_in_bounds")
    products = jnp.einsum("dtr,trc->dtc", picked, tile_grp, preferred_element_type=jnp.float32)
    onehot = (
        (src_grp[:, None] == jnp.arange(src_blocks, dtype=jnp.int32)[None, :]) & live_mask[:, None]
    ).astype(jnp.float32)
    return jnp.einsum("dtc,ts->dsc", products, onehot)


def over_tiles(kernel, source, tile_values, tile_dst, tile_src, tile_total, out_blocks):
    capacity = tile_values.shape[0]
    live_mask = jnp.arange(capacity, dtype=jnp.int32) < tile_total
    return kernel(source, tile_values, tile_dst, tile_src, live_mask, out_blocks)


def bf16_parts(x, count):
    parts = []
    rest = x
    for _ in range(count - 1):
        head = lax.reduce_precision(rest, exponent_bits=8, mantissa_bits=7)
        parts.append(head.astype(jnp.bfloat16))
        rest = rest - head
    parts.append(rest.astype(jnp.bfloat16))
    return parts


def parts_sum(parts):
    total = parts[0].astype(jnp.float32)
    for part in parts[1:]:
        total = total + part.astype(jnp.float32)
    return total


def local(
    states,
    depth_weight,
    tile_values,
    tile_dst,
    tile_src,
    tile_count,
    send_rows,
    weight,
    bias_vec,
    cotangent,
):
    f32 = jnp.float32
    bf16 = jnp.bfloat16
    channels = states.shape[1]
    row_count = states.shape[2]
    block_size = tile_values.shape[2]
    row_blocks = row_count // block_size
    my_tiles = tile_values[0]
    my_dst = tile_dst[0]
    my_src = tile_src[0]
    tile_total = tile_count[0]
    my_send = send_rows[0]
    section_count = my_send.shape[0]
    halo_width = my_send.shape[1]
    vert_count = lax.axis_size("vert")
    feat_count = lax.axis_size("feat")
    col_width = row_count // feat_count
    width = weight.shape[1]
    src_blocks = (row_count + section_count * halo_width) // block_size
    norm_scale = 1.0 / math.sqrt(vert_count * row_count)

    def to_blocks(x):
        return x.reshape(channels, feat_count, col_width).transpose(1, 0, 2)

    def from_blocks(x):
        return x.transpose(1, 0, 2).reshape(channels, row_count)

    state_count = states.shape[0]
    listed = (
        states.reshape(state_count * channels, row_count)
        .at[:, my_send.reshape(-1)]
        .get(mode="promise_in_bounds")
    )
    halo_states = lax.all_to_all(
        listed.reshape(state_count, channels, section_count, halo_width),
        "vert",
        split_axis=2,
        concat_axis=2,
        tiled=True,
    )
    mixed_state = jnp.sum(depth_weight[:, :, None] * states, axis=0).astype(bf16)
    mixed_halo = jnp.sum(depth_weight[:, :, None, None] * halo_states, axis=0).astype(bf16)
    extended = jnp.concatenate([mixed_state, mixed_halo.reshape(channels, -1)], axis=1)
    extended = extended.reshape(channels, src_blocks, block_size)
    aggregated = over_tiles(
        tile_forward, extended, my_tiles, my_dst, my_src, tile_total, row_blocks
    )
    aggregated = aggregated.reshape(channels, row_count).astype(bf16)

    bias_cols = jnp.broadcast_to(
        jnp.stack(bf16_parts(bias_vec, 3), axis=1)[None], (feat_count, channels, 3)
    )
    first_send = jnp.concatenate([to_blocks(aggregated), to_blocks(cotangent), bias_cols], axis=2)
    first_recv = lax.all_to_all(first_send, "feat", split_axis=0, concat_axis=0, tiled=True)
    first_recv = first_recv.reshape(feat_count * channels, -1)
    agg_block = first_recv[:, :col_width]
    cot_block = first_recv[:, col_width : 2 * col_width].astype(f32)
    bias_full = parts_sum([first_recv[:, 2 * col_width + n] for n in range(3)])

    pre_act = lax.dot_general(
        weight, agg_block, (((0,), (0,)), ((), ())), preferred_element_type=f32
    )
    pre_act = pre_act + bias_full[:, None]
    sigmoid_pre = jax.nn.sigmoid(pre_act)
    out_block = (pre_act * sigmoid_pre).astype(bf16)
    grad_pre = (cot_block * sigmoid_pre * (1.0 + pre_act * (1.0 - sigmoid_pre))).astype(bf16)
    grad_agg_block = jnp.dot(weight, grad_pre, preferred_element_type=f32).astype(bf16)
    weight_terms = lax.dot_general(
        agg_block, grad_pre, (((1,), (1,)), ((), ())), preferred_element_type=f32
    )
    bias_terms = jnp.sum(grad_pre.astype(f32), axis=1)

    grad_terms = jnp.concatenate(
        [
            weight_terms.reshape(feat_count, channels, width),
            bias_terms.reshape(feat_count, channels, 1),
        ],
        axis=2,
    )
    second_send = jnp.concatenate(
        [
            out_block.reshape(feat_count, channels, col_width),
            grad_agg_block.reshape(feat_count, channels, col_width),
        ]
        + bf16_parts(grad_terms, 1),
        axis=2,
    )
    second_recv = lax.all_to_all(second_send, "feat", split_axis=0, concat_axis=0, tiled=True)
    layer_out = from_blocks(second_recv[:, :, :col_width])
    grad_agg = from_blocks(second_recv[:, :, col_width : 2 * col_width])
    terms_width = width + 1
    start = 2 * col_width
    panel_terms = jnp.sum(second_recv[:, :, start : start + terms_width].astype(f32), axis=0)

    grad_blocks = grad_agg.reshape(channels, row_blocks, block_size)
    spread_out = over_tiles(
        tile_backward, grad_blocks, my_tiles, my_dst, my_src, tile_total, src_blocks
    )
    spread_out = spread_out.reshape(channels, src_blocks * block_size)
    own_grad = spread_out[:, :row_count]
    halo_part = spread_out[:, row_count:].reshape(channels, section_count, halo_width)
    halo_terms = lax.reduce_precision(halo_part, exponent_bits=8, mantissa_bits=7)
    depth_terms = jnp.sum(states * own_grad[None], axis=2) + jnp.sum(
        halo_states * halo_terms[None], axis=(2, 3)
    )
    totals = jnp.concatenate([panel_terms.reshape(-1), depth_terms.reshape(-1)]) * norm_scale
    last_send = jnp.concatenate(
        [halo_part.astype(bf16).transpose(1, 0, 2).reshape(section_count, channels * halo_width)]
        + [
            jnp.broadcast_to(part[None, :], (vert_count, totals.shape[0]))
            for part in bf16_parts(totals, 1)
        ],
        axis=1,
    )
    last_recv = lax.all_to_all(last_send, "vert", split_axis=0, concat_axis=0, tiled=True)
    returned = (
        last_recv[:, : channels * halo_width]
        .reshape(section_count, channels, halo_width)
        .transpose(1, 0, 2)
    )
    tail = last_recv[:, channels * halo_width :]
    totals = jnp.sum(tail.astype(f32), axis=0)
    hot = (
        my_send.reshape(-1)[None, :] == jnp.arange(row_count, dtype=jnp.int32)[:, None]
    ).astype(bf16)
    added = lax.dot_general(
        hot,
        returned.reshape(channels, -1),
        (((1,), (1,)), ((), ())),
        preferred_element_type=f32,
    )
    grad_mixed = own_grad + added.T
    grad_states = (depth_weight[:, :, None] * grad_mixed[None]).astype(bf16)
    panel_sum = totals[: panel_terms.size].reshape(panel_terms.shape)
    depth_sum = totals[panel_terms.size :].reshape(depth_terms.shape)
    return (
        layer_out,
        grad_states,
        panel_sum[:, :width],
        panel_sum[:, width],
        depth_sum,
    )


def solution(mesh):
    placed = (
        P(None, "feat", "vert"),
        P(None, "feat"),
        P("vert", None, None, None),
        P("vert", None),
        P("vert", None),
        P("vert"),
        P("vert", None, None),
        P(),
        P("feat"),
        P("feat", "vert"),
    )
    return jax.shard_map(
        local,
        mesh=mesh,
        in_specs=placed,
        out_specs=(
            P("feat", "vert"),
            P(None, "feat", "vert"),
            P("feat", None),
            P("feat"),
            P(None, "feat"),
        ),
        check_vma=False,
    )
```

```python
import math

import jax
import jax.numpy as jnp
from jax import lax
from jax.sharding import PartitionSpec as P


def tile_forward(extended, tile_grp, dst_grp, src_grp, live_mask, row_blocks):
    picked = extended.at[:, src_grp].get(mode="promise_in_bounds")
    products = jnp.einsum("dtc,trc->dtr", picked, tile_grp, preferred_element_type=jnp.float32)
    onehot = (
        (dst_grp[:, None] == jnp.arange(row_blocks, dtype=jnp.int32)[None, :]) & live_mask[:, None]
    ).astype(jnp.float32)
    return jnp.einsum("dtr,tn->dnr", products, onehot)


def tile_backward(grad_blocks, tile_grp, dst_grp, src_grp, live_mask, src_blocks):
    picked = grad_blocks.at[:, dst_grp].get(mode="promise_in_bounds")
    products = jnp.einsum("dtr,trc->dtc", picked, tile_grp, preferred_element_type=jnp.float32)
    onehot = (
        (src_grp[:, None] == jnp.arange(src_blocks, dtype=jnp.int32)[None, :]) & live_mask[:, None]
    ).astype(jnp.float32)
    return jnp.einsum("dtc,ts->dsc", products, onehot)


def over_tiles(kernel, source, tile_values, tile_dst, tile_src, tile_total, out_blocks):
    capacity = tile_values.shape[0]
    live_mask = jnp.arange(capacity, dtype=jnp.int32) < tile_total
    return kernel(source, tile_values, tile_dst, tile_src, live_mask, out_blocks)


def bf16_parts(x, count):
    parts = []
    rest = x
    for _ in range(count - 1):
        head = lax.reduce_precision(rest, exponent_bits=8, mantissa_bits=7)
        parts.append(head.astype(jnp.bfloat16))
        rest = rest - head
    parts.append(rest.astype(jnp.bfloat16))
    return parts


def parts_sum(parts):
    total = parts[0].astype(jnp.float32)
    for part in parts[1:]:
        total = total + part.astype(jnp.float32)
    return total


def local(
    states,
    depth_weight,
    tile_values,
    tile_dst,
    tile_src,
    tile_count,
    send_rows,
    weight,
    bias_vec,
    cotangent,
):
    f32 = jnp.float32
    bf16 = jnp.bfloat16
    channels = states.shape[1]
    row_count = states.shape[2]
    block_size = tile_values.shape[2]
    row_blocks = row_count // block_size
    my_tiles = tile_values[0]
    my_dst = tile_dst[0]
    my_src = tile_src[0]
    tile_total = tile_count[0]
    my_send = send_rows[0]
    section_count = my_send.shape[0]
    halo_width = my_send.shape[1]
    vert_count = lax.axis_size("vert")
    feat_count = lax.axis_size("feat")
    col_width = row_count // feat_count
    width = weight.shape[1]
    src_blocks = (row_count + section_count * halo_width) // block_size
    norm_scale = 1.0 / math.sqrt(vert_count * row_count)

    def to_blocks(x):
        return x.reshape(channels, feat_count, col_width).transpose(1, 0, 2)

    def from_blocks(x):
        return x.transpose(1, 0, 2).reshape(channels, row_count)

    state_count = states.shape[0]
    listed = (
        states.reshape(state_count * channels, row_count)
        .at[:, my_send.reshape(-1)]
        .get(mode="promise_in_bounds")
    )
    halo_states = lax.all_to_all(
        listed.reshape(state_count, channels, section_count, halo_width),
        "vert",
        split_axis=2,
        concat_axis=2,
        tiled=True,
    )
    mixed_state = jnp.sum(depth_weight[:, :, None] * states, axis=0).astype(bf16)
    mixed_halo = jnp.sum(depth_weight[:, :, None, None] * halo_states, axis=0).astype(bf16)
    extended = jnp.concatenate([mixed_state, mixed_halo.reshape(channels, -1)], axis=1)
    extended = extended.reshape(channels, src_blocks, block_size)
    aggregated = over_tiles(
        tile_forward, extended, my_tiles, my_dst, my_src, tile_total, row_blocks
    )
    aggregated = aggregated.reshape(channels, row_count).astype(bf16)

    bias_cols = jnp.broadcast_to(
        jnp.stack(bf16_parts(bias_vec, 3), axis=1)[None], (feat_count, channels, 3)
    )
    first_send = jnp.concatenate([to_blocks(aggregated), to_blocks(cotangent), bias_cols], axis=2)
    first_recv = lax.all_to_all(first_send, "feat", split_axis=0, concat_axis=0, tiled=True)
    first_recv = first_recv.reshape(feat_count * channels, -1)
    agg_block = first_recv[:, :col_width]
    cot_block = first_recv[:, col_width : 2 * col_width].astype(f32)
    bias_full = parts_sum([first_recv[:, 2 * col_width + n] for n in range(3)])

    pre_act = lax.dot_general(
        weight, agg_block, (((0,), (0,)), ((), ())), preferred_element_type=f32
    )
    pre_act = pre_act + bias_full[:, None]
    sigmoid_pre = jax.nn.sigmoid(pre_act)
    out_block = (pre_act * sigmoid_pre).astype(bf16)
    grad_pre = (cot_block * sigmoid_pre * (1.0 + pre_act * (1.0 - sigmoid_pre))).astype(bf16)
    grad_agg_block = jnp.dot(weight, grad_pre, preferred_element_type=f32).astype(bf16)
    weight_terms = lax.dot_general(
        agg_block, grad_pre, (((1,), (1,)), ((), ())), preferred_element_type=f32
    )
    bias_terms = jnp.sum(grad_pre.astype(f32), axis=1)

    second_send = jnp.concatenate(
        [
            out_block.reshape(feat_count, channels, col_width),
            grad_agg_block.reshape(feat_count, channels, col_width),
            weight_terms.reshape(feat_count, channels, width).astype(bf16),
        ]
        + bf16_parts(bias_terms.reshape(feat_count, channels, 1), 2),
        axis=2,
    )
    second_recv = lax.all_to_all(second_send, "feat", split_axis=0, concat_axis=0, tiled=True)
    layer_out = from_blocks(second_recv[:, :, :col_width])
    grad_agg = from_blocks(second_recv[:, :, col_width : 2 * col_width])
    start = 2 * col_width
    weight_part = second_recv[:, :, start : start + width].astype(f32)
    bias_part = parts_sum(
        [second_recv[:, :, start + width : start + width + 1], second_recv[:, :, start + width + 1 :]]
    )
    panel_terms = jnp.sum(jnp.concatenate([weight_part, bias_part], axis=2), axis=0)

    grad_blocks = grad_agg.reshape(channels, row_blocks, block_size)
    spread_out = over_tiles(
        tile_backward, grad_blocks, my_tiles, my_dst, my_src, tile_total, src_blocks
    )
    spread_out = spread_out.reshape(channels, src_blocks * block_size)
    own_grad = spread_out[:, :row_count]
    halo_part = spread_out[:, row_count:].reshape(channels, section_count, halo_width)
    halo_terms = lax.reduce_precision(halo_part, exponent_bits=8, mantissa_bits=7)
    depth_terms = jnp.sum(states * own_grad[None], axis=2) + jnp.sum(
        halo_states * halo_terms[None], axis=(2, 3)
    )
    weight_total = panel_terms[:, :width].reshape(-1) * norm_scale
    small_total = (
        jnp.concatenate([panel_terms[:, width], depth_terms.reshape(-1)]) * norm_scale
    )
    last_send = jnp.concatenate(
        [halo_part.astype(bf16).transpose(1, 0, 2).reshape(section_count, channels * halo_width)]
        + [
            jnp.broadcast_to(part[None, :], (vert_count, part.shape[0]))
            for part in [weight_total.astype(bf16)] + bf16_parts(small_total, 2)
        ],
        axis=1,
    )
    last_recv = lax.all_to_all(last_send, "vert", split_axis=0, concat_axis=0, tiled=True)
    returned = (
        last_recv[:, : channels * halo_width]
        .reshape(section_count, channels, halo_width)
        .transpose(1, 0, 2)
    )
    tail = last_recv[:, channels * halo_width :]
    weight_count = weight_total.shape[0]
    small_count = small_total.shape[0]
    weight_sum = jnp.sum(tail[:, :weight_count].astype(f32), axis=0)
    small_sum = jnp.sum(
        parts_sum(
            [
                tail[:, weight_count : weight_count + small_count],
                tail[:, weight_count + small_count :],
            ]
        ),
        axis=0,
    )
    hot = (
        my_send.reshape(-1)[None, :] == jnp.arange(row_count, dtype=jnp.int32)[:, None]
    ).astype(bf16)
    added = lax.dot_general(
        hot,
        returned.reshape(channels, -1),
        (((1,), (1,)), ((), ())),
        preferred_element_type=f32,
    )
    grad_mixed = own_grad + added.T
    grad_states = (depth_weight[:, :, None] * grad_mixed[None]).astype(bf16)
    return (
        layer_out,
        grad_states,
        weight_sum.reshape(channels, width),
        small_sum[:channels],
        small_sum[channels:].reshape(depth_terms.shape),
    )


def solution(mesh):
    placed = (
        P(None, "feat", "vert"),
        P(None, "feat"),
        P("vert", None, None, None),
        P("vert", None),
        P("vert", None),
        P("vert"),
        P("vert", None, None),
        P(),
        P("feat"),
        P("feat", "vert"),
    )
    return jax.shard_map(
        local,
        mesh=mesh,
        in_specs=placed,
        out_specs=(
            P("feat", "vert"),
            P(None, "feat", "vert"),
            P("feat", None),
            P("feat"),
            P(None, "feat"),
        ),
        check_vma=False,
    )
```

```python
import math

import jax
import jax.numpy as jnp
from jax import lax
from jax.sharding import PartitionSpec as P


def tile_forward(extended, tile_grp, dst_grp, src_grp, live_mask, row_blocks):
    picked = extended.at[:, src_grp].get(mode="promise_in_bounds")
    products = jnp.einsum("dtc,trc->dtr", picked, tile_grp, preferred_element_type=jnp.float32)
    onehot = (
        (dst_grp[:, None] == jnp.arange(row_blocks, dtype=jnp.int32)[None, :]) & live_mask[:, None]
    ).astype(jnp.float32)
    return jnp.einsum("dtr,tn->dnr", products, onehot)


def tile_backward(grad_blocks, tile_grp, dst_grp, src_grp, live_mask, src_blocks):
    picked = grad_blocks.at[:, dst_grp].get(mode="promise_in_bounds")
    products = jnp.einsum("dtr,trc->dtc", picked, tile_grp, preferred_element_type=jnp.float32)
    onehot = (
        (src_grp[:, None] == jnp.arange(src_blocks, dtype=jnp.int32)[None, :]) & live_mask[:, None]
    ).astype(jnp.float32)
    return jnp.einsum("dtc,ts->dsc", products, onehot)


def over_tiles(kernel, source, tile_values, tile_dst, tile_src, tile_total, out_blocks):
    capacity = tile_values.shape[0]
    live_mask = jnp.arange(capacity, dtype=jnp.int32) < tile_total
    return kernel(source, tile_values, tile_dst, tile_src, live_mask, out_blocks)


def bf16_parts(x, count):
    parts = []
    rest = x
    for _ in range(count - 1):
        head = lax.reduce_precision(rest, exponent_bits=8, mantissa_bits=7)
        parts.append(head.astype(jnp.bfloat16))
        rest = rest - head
    parts.append(rest.astype(jnp.bfloat16))
    return parts


def parts_sum(parts):
    total = parts[0].astype(jnp.float32)
    for part in parts[1:]:
        total = total + part.astype(jnp.float32)
    return total


def local(
    states,
    depth_weight,
    tile_values,
    tile_dst,
    tile_src,
    tile_count,
    send_rows,
    weight,
    bias_vec,
    cotangent,
):
    f32 = jnp.float32
    bf16 = jnp.bfloat16
    channels = states.shape[1]
    row_count = states.shape[2]
    block_size = tile_values.shape[2]
    row_blocks = row_count // block_size
    my_tiles = tile_values[0]
    my_dst = tile_dst[0]
    my_src = tile_src[0]
    tile_total = tile_count[0]
    my_send = send_rows[0]
    section_count = my_send.shape[0]
    halo_width = my_send.shape[1]
    vert_count = lax.axis_size("vert")
    feat_count = lax.axis_size("feat")
    col_width = row_count // feat_count
    width = weight.shape[1]
    src_blocks = (row_count + section_count * halo_width) // block_size
    norm_scale = 1.0 / math.sqrt(vert_count * row_count)

    def to_blocks(x):
        return x.reshape(channels, feat_count, col_width).transpose(1, 0, 2)

    def from_blocks(x):
        return x.transpose(1, 0, 2).reshape(channels, row_count)

    state_count = states.shape[0]
    pick = (
        my_send.reshape(-1)[:, None] == jnp.arange(row_count, dtype=jnp.int32)[None, :]
    ).astype(bf16)
    listed = (
        lax.dot_general(
            pick,
            states.reshape(state_count * channels, row_count),
            (((1,), (1,)), ((), ())),
            preferred_element_type=f32,
        )
        .astype(bf16)
        .T
    )
    halo_states = lax.all_to_all(
        listed.reshape(state_count, channels, section_count, halo_width),
        "vert",
        split_axis=2,
        concat_axis=2,
        tiled=True,
    )
    mixed_state = jnp.sum(depth_weight[:, :, None] * states, axis=0).astype(bf16)
    mixed_halo = jnp.sum(depth_weight[:, :, None, None] * halo_states, axis=0).astype(bf16)
    extended = jnp.concatenate([mixed_state, mixed_halo.reshape(channels, -1)], axis=1)
    extended = extended.reshape(channels, src_blocks, block_size)
    aggregated = over_tiles(
        tile_forward, extended, my_tiles, my_dst, my_src, tile_total, row_blocks
    )
    aggregated = aggregated.reshape(channels, row_count).astype(bf16)

    bias_cols = jnp.broadcast_to(
        jnp.stack(bf16_parts(bias_vec, 3), axis=1)[None], (feat_count, channels, 3)
    )
    first_send = jnp.concatenate([to_blocks(aggregated), to_blocks(cotangent), bias_cols], axis=2)
    first_recv = lax.all_to_all(first_send, "feat", split_axis=0, concat_axis=0, tiled=True)
    first_recv = first_recv.reshape(feat_count * channels, -1)
    agg_block = first_recv[:, :col_width]
    cot_block = first_recv[:, col_width : 2 * col_width].astype(f32)
    bias_full = parts_sum([first_recv[:, 2 * col_width + n] for n in range(3)])

    pre_act = lax.dot_general(
        weight, agg_block, (((0,), (0,)), ((), ())), preferred_element_type=f32
    )
    pre_act = pre_act + bias_full[:, None]
    sigmoid_pre = jax.nn.sigmoid(pre_act)
    out_block = (pre_act * sigmoid_pre).astype(bf16)
    grad_pre = (cot_block * sigmoid_pre * (1.0 + pre_act * (1.0 - sigmoid_pre))).astype(bf16)
    grad_agg_block = jnp.dot(weight, grad_pre, preferred_element_type=f32).astype(bf16)
    weight_terms = lax.dot_general(
        agg_block, grad_pre, (((1,), (1,)), ((), ())), preferred_element_type=f32
    )
    bias_terms = jnp.sum(grad_pre.astype(f32), axis=1)

    second_send = jnp.concatenate(
        [
            out_block.reshape(feat_count, channels, col_width),
            grad_agg_block.reshape(feat_count, channels, col_width),
            weight_terms.reshape(feat_count, channels, width).astype(bf16),
        ]
        + bf16_parts(bias_terms.reshape(feat_count, channels, 1), 2),
        axis=2,
    )
    second_recv = lax.all_to_all(second_send, "feat", split_axis=0, concat_axis=0, tiled=True)
    layer_out = from_blocks(second_recv[:, :, :col_width])
    grad_agg = from_blocks(second_recv[:, :, col_width : 2 * col_width])
    start = 2 * col_width
    weight_part = second_recv[:, :, start : start + width].astype(f32)
    bias_part = parts_sum(
        [second_recv[:, :, start + width : start + width + 1], second_recv[:, :, start + width + 1 :]]
    )
    panel_terms = jnp.sum(jnp.concatenate([weight_part, bias_part], axis=2), axis=0)

    grad_blocks = grad_agg.reshape(channels, row_blocks, block_size)
    spread_out = over_tiles(
        tile_backward, grad_blocks, my_tiles, my_dst, my_src, tile_total, src_blocks
    )
    spread_out = spread_out.reshape(channels, src_blocks * block_size)
    own_grad = spread_out[:, :row_count]
    halo_part = spread_out[:, row_count:].reshape(channels, section_count, halo_width)
    halo_terms = lax.reduce_precision(halo_part, exponent_bits=8, mantissa_bits=7)
    depth_terms = jnp.sum(states * own_grad[None], axis=2) + jnp.sum(
        halo_states * halo_terms[None], axis=(2, 3)
    )
    weight_total = panel_terms[:, :width].reshape(-1) * norm_scale
    small_total = (
        jnp.concatenate([panel_terms[:, width], depth_terms.reshape(-1)]) * norm_scale
    )
    last_send = jnp.concatenate(
        [halo_part.astype(bf16).transpose(1, 0, 2).reshape(section_count, channels * halo_width)]
        + [
            jnp.broadcast_to(part[None, :], (vert_count, part.shape[0]))
            for part in [weight_total.astype(bf16)] + bf16_parts(small_total, 2)
        ],
        axis=1,
    )
    last_recv = lax.all_to_all(last_send, "vert", split_axis=0, concat_axis=0, tiled=True)
    returned = (
        last_recv[:, : channels * halo_width]
        .reshape(section_count, channels, halo_width)
        .transpose(1, 0, 2)
    )
    tail = last_recv[:, channels * halo_width :]
    weight_count = weight_total.shape[0]
    small_count = small_total.shape[0]
    weight_sum = jnp.sum(tail[:, :weight_count].astype(f32), axis=0)
    small_sum = jnp.sum(
        parts_sum(
            [
                tail[:, weight_count : weight_count + small_count],
                tail[:, weight_count + small_count :],
            ]
        ),
        axis=0,
    )
    hot = (
        my_send.reshape(-1)[None, :] == jnp.arange(row_count, dtype=jnp.int32)[:, None]
    ).astype(bf16)
    added = lax.dot_general(
        hot,
        returned.reshape(channels, -1),
        (((1,), (1,)), ((), ())),
        preferred_element_type=f32,
    )
    grad_mixed = own_grad + added.T
    grad_states = (depth_weight[:, :, None] * grad_mixed[None]).astype(bf16)
    return (
        layer_out,
        grad_states,
        weight_sum.reshape(channels, width),
        small_sum[:channels],
        small_sum[channels:].reshape(depth_terms.shape),
    )


def solution(mesh):
    placed = (
        P(None, "feat", "vert"),
        P(None, "feat"),
        P("vert", None, None, None),
        P("vert", None),
        P("vert", None),
        P("vert"),
        P("vert", None, None),
        P(),
        P("feat"),
        P("feat", "vert"),
    )
    return jax.shard_map(
        local,
        mesh=mesh,
        in_specs=placed,
        out_specs=(
            P("feat", "vert"),
            P(None, "feat", "vert"),
            P("feat", None),
            P("feat"),
            P(None, "feat"),
        ),
        check_vma=False,
    )
```

```python
import math

import jax
import jax.numpy as jnp
from jax import lax
from jax.sharding import PartitionSpec as P


def tile_forward(extended, tile_grp, dst_grp, src_grp, live_mask, row_blocks):
    picked = extended.at[:, src_grp].get(mode="promise_in_bounds")
    products = jnp.einsum("dtc,trc->dtr", picked, tile_grp, preferred_element_type=jnp.float32)
    onehot = (
        (dst_grp[:, None] == jnp.arange(row_blocks, dtype=jnp.int32)[None, :]) & live_mask[:, None]
    ).astype(jnp.float32)
    return jnp.einsum("dtr,tn->dnr", products, onehot)


def tile_backward(grad_blocks, tile_grp, dst_grp, src_grp, live_mask, src_blocks):
    picked = grad_blocks.at[:, dst_grp].get(mode="promise_in_bounds")
    products = jnp.einsum("dtr,trc->dtc", picked, tile_grp, preferred_element_type=jnp.float32)
    onehot = (
        (src_grp[:, None] == jnp.arange(src_blocks, dtype=jnp.int32)[None, :]) & live_mask[:, None]
    ).astype(jnp.float32)
    return jnp.einsum("dtc,ts->dsc", products, onehot)


def over_tiles(kernel, source, tile_values, tile_dst, tile_src, tile_total, out_blocks):
    capacity = tile_values.shape[0]
    live_mask = jnp.arange(capacity, dtype=jnp.int32) < tile_total
    return kernel(source, tile_values, tile_dst, tile_src, live_mask, out_blocks)


def bf16_parts(x, count):
    parts = []
    rest = x
    for _ in range(count - 1):
        head = lax.reduce_precision(rest, exponent_bits=8, mantissa_bits=7)
        parts.append(head.astype(jnp.bfloat16))
        rest = rest - head
    parts.append(rest.astype(jnp.bfloat16))
    return parts


def parts_sum(parts):
    total = parts[0].astype(jnp.float32)
    for part in parts[1:]:
        total = total + part.astype(jnp.float32)
    return total


def local(
    states,
    depth_weight,
    tile_values,
    tile_dst,
    tile_src,
    tile_count,
    send_rows,
    weight,
    bias_vec,
    cotangent,
):
    f32 = jnp.float32
    bf16 = jnp.bfloat16
    channels = states.shape[1]
    row_count = states.shape[2]
    block_size = tile_values.shape[2]
    row_blocks = row_count // block_size
    my_tiles = tile_values[0]
    my_dst = tile_dst[0]
    my_src = tile_src[0]
    tile_total = tile_count[0]
    my_send = send_rows[0]
    section_count = my_send.shape[0]
    halo_width = my_send.shape[1]
    vert_count = lax.axis_size("vert")
    feat_count = lax.axis_size("feat")
    col_width = row_count // feat_count
    width = weight.shape[1]
    src_blocks = (row_count + section_count * halo_width) // block_size
    norm_scale = 1.0 / math.sqrt(vert_count * row_count)

    def to_blocks(x):
        return x.reshape(channels, feat_count, col_width).transpose(1, 0, 2)

    def from_blocks(x):
        return x.transpose(1, 0, 2).reshape(channels, row_count)

    state_count = states.shape[0]
    pick = (
        jnp.arange(row_count, dtype=jnp.int32)[:, None] == my_send.reshape(-1)[None, :]
    ).astype(bf16)
    listed = jnp.dot(
        states.reshape(state_count * channels, row_count), pick, preferred_element_type=f32
    ).astype(bf16)
    halo_states = lax.all_to_all(
        listed.reshape(state_count, channels, section_count, halo_width),
        "vert",
        split_axis=2,
        concat_axis=2,
        tiled=True,
    )
    mixed_state = jnp.sum(depth_weight[:, :, None] * states, axis=0).astype(bf16)
    mixed_halo = jnp.sum(depth_weight[:, :, None, None] * halo_states, axis=0).astype(bf16)
    extended = jnp.concatenate([mixed_state, mixed_halo.reshape(channels, -1)], axis=1)
    extended = extended.reshape(channels, src_blocks, block_size)
    aggregated = over_tiles(
        tile_forward, extended, my_tiles, my_dst, my_src, tile_total, row_blocks
    )
    aggregated = aggregated.reshape(channels, row_count).astype(bf16)

    bias_cols = jnp.broadcast_to(
        jnp.stack(bf16_parts(bias_vec, 3), axis=1)[None], (feat_count, channels, 3)
    )
    first_send = jnp.concatenate([to_blocks(aggregated), to_blocks(cotangent), bias_cols], axis=2)
    first_recv = lax.all_to_all(first_send, "feat", split_axis=0, concat_axis=0, tiled=True)
    first_recv = first_recv.reshape(feat_count * channels, -1)
    agg_block = first_recv[:, :col_width]
    cot_block = first_recv[:, col_width : 2 * col_width].astype(f32)
    bias_full = parts_sum([first_recv[:, 2 * col_width + n] for n in range(3)])

    pre_act = lax.dot_general(
        weight, agg_block, (((0,), (0,)), ((), ())), preferred_element_type=f32
    )
    pre_act = pre_act + bias_full[:, None]
    sigmoid_pre = jax.nn.sigmoid(pre_act)
    out_block = (pre_act * sigmoid_pre).astype(bf16)
    grad_pre = (cot_block * sigmoid_pre * (1.0 + pre_act * (1.0 - sigmoid_pre))).astype(bf16)
    grad_agg_block = jnp.dot(weight, grad_pre, preferred_element_type=f32).astype(bf16)
    weight_terms = lax.dot_general(
        agg_block, grad_pre, (((1,), (1,)), ((), ())), preferred_element_type=f32
    )
    bias_terms = jnp.sum(grad_pre.astype(f32), axis=1)

    second_send = jnp.concatenate(
        [
            out_block.reshape(feat_count, channels, col_width),
            grad_agg_block.reshape(feat_count, channels, col_width),
            weight_terms.reshape(feat_count, channels, width).astype(bf16),
        ]
        + bf16_parts(bias_terms.reshape(feat_count, channels, 1), 2),
        axis=2,
    )
    second_recv = lax.all_to_all(second_send, "feat", split_axis=0, concat_axis=0, tiled=True)
    layer_out = from_blocks(second_recv[:, :, :col_width])
    grad_agg = from_blocks(second_recv[:, :, col_width : 2 * col_width])
    start = 2 * col_width
    weight_part = second_recv[:, :, start : start + width].astype(f32)
    bias_part = parts_sum(
        [second_recv[:, :, start + width : start + width + 1], second_recv[:, :, start + width + 1 :]]
    )
    panel_terms = jnp.sum(jnp.concatenate([weight_part, bias_part], axis=2), axis=0)

    grad_blocks = grad_agg.reshape(channels, row_blocks, block_size)
    spread_out = over_tiles(
        tile_backward, grad_blocks, my_tiles, my_dst, my_src, tile_total, src_blocks
    )
    spread_out = spread_out.reshape(channels, src_blocks * block_size)
    own_grad = spread_out[:, :row_count]
    halo_part = spread_out[:, row_count:].reshape(channels, section_count, halo_width)
    halo_terms = lax.reduce_precision(halo_part, exponent_bits=8, mantissa_bits=7)
    depth_terms = jnp.sum(states * own_grad[None], axis=2) + jnp.sum(
        halo_states * halo_terms[None], axis=(2, 3)
    )
    weight_total = panel_terms[:, :width].reshape(-1) * norm_scale
    small_total = (
        jnp.concatenate([panel_terms[:, width], depth_terms.reshape(-1)]) * norm_scale
    )
    last_send = jnp.concatenate(
        [halo_part.astype(bf16).transpose(1, 0, 2).reshape(section_count, channels * halo_width)]
        + [
            jnp.broadcast_to(part[None, :], (vert_count, part.shape[0]))
            for part in [weight_total.astype(bf16)] + bf16_parts(small_total, 2)
        ],
        axis=1,
    )
    last_recv = lax.all_to_all(last_send, "vert", split_axis=0, concat_axis=0, tiled=True)
    returned = (
        last_recv[:, : channels * halo_width]
        .reshape(section_count, channels, halo_width)
        .transpose(1, 0, 2)
    )
    tail = last_recv[:, channels * halo_width :]
    weight_count = weight_total.shape[0]
    small_count = small_total.shape[0]
    weight_sum = jnp.sum(tail[:, :weight_count].astype(f32), axis=0)
    small_sum = jnp.sum(
        parts_sum(
            [
                tail[:, weight_count : weight_count + small_count],
                tail[:, weight_count + small_count :],
            ]
        ),
        axis=0,
    )
    hot = (
        my_send.reshape(-1)[None, :] == jnp.arange(row_count, dtype=jnp.int32)[:, None]
    ).astype(bf16)
    added = lax.dot_general(
        hot,
        returned.reshape(channels, -1),
        (((1,), (1,)), ((), ())),
        preferred_element_type=f32,
    )
    grad_mixed = own_grad + added.T
    grad_states = (depth_weight[:, :, None] * grad_mixed[None]).astype(bf16)
    return (
        layer_out,
        grad_states,
        weight_sum.reshape(channels, width),
        small_sum[:channels],
        small_sum[channels:].reshape(depth_terms.shape),
    )


def solution(mesh):
    placed = (
        P(None, "feat", "vert"),
        P(None, "feat"),
        P("vert", None, None, None),
        P("vert", None),
        P("vert", None),
        P("vert"),
        P("vert", None, None),
        P(),
        P("feat"),
        P("feat", "vert"),
    )
    return jax.shard_map(
        local,
        mesh=mesh,
        in_specs=placed,
        out_specs=(
            P("feat", "vert"),
            P(None, "feat", "vert"),
            P("feat", None),
            P("feat"),
            P(None, "feat"),
        ),
        check_vma=False,
    )
```

```python
import math

import jax
import jax.numpy as jnp
from jax import lax
from jax.sharding import PartitionSpec as P


def tile_forward(extended, tile_grp, dst_grp, src_grp, live_mask, row_blocks):
    picked = extended.at[:, src_grp].get(mode="promise_in_bounds")
    products = jnp.einsum("dtc,trc->dtr", picked, tile_grp, preferred_element_type=jnp.float32)
    onehot = (
        (dst_grp[:, None] == jnp.arange(row_blocks, dtype=jnp.int32)[None, :]) & live_mask[:, None]
    ).astype(jnp.float32)
    return jnp.einsum("dtr,tn->dnr", products, onehot)


def tile_backward(grad_blocks, tile_grp, dst_grp, src_grp, live_mask, src_blocks):
    picked = grad_blocks.at[:, dst_grp].get(mode="promise_in_bounds")
    products = jnp.einsum("dtr,trc->dtc", picked, tile_grp, preferred_element_type=jnp.float32)
    onehot = (
        (src_grp[:, None] == jnp.arange(src_blocks, dtype=jnp.int32)[None, :]) & live_mask[:, None]
    ).astype(jnp.float32)
    return jnp.einsum("dtc,ts->dsc", products, onehot)


def over_tiles(kernel, source, tile_values, tile_dst, tile_src, tile_total, out_blocks):
    capacity = tile_values.shape[0]
    live_mask = jnp.arange(capacity, dtype=jnp.int32) < tile_total
    return kernel(source, tile_values, tile_dst, tile_src, live_mask, out_blocks)


def bf16_parts(x, count):
    parts = []
    rest = x
    for _ in range(count - 1):
        head = lax.reduce_precision(rest, exponent_bits=8, mantissa_bits=7)
        parts.append(head.astype(jnp.bfloat16))
        rest = rest - head
    parts.append(rest.astype(jnp.bfloat16))
    return parts


def parts_sum(parts):
    total = parts[0].astype(jnp.float32)
    for part in parts[1:]:
        total = total + part.astype(jnp.float32)
    return total


def local(
    states,
    depth_weight,
    tile_values,
    tile_dst,
    tile_src,
    tile_count,
    send_rows,
    weight,
    bias_vec,
    cotangent,
):
    f32 = jnp.float32
    bf16 = jnp.bfloat16
    channels = states.shape[1]
    row_count = states.shape[2]
    block_size = tile_values.shape[2]
    row_blocks = row_count // block_size
    my_tiles = tile_values[0]
    my_dst = tile_dst[0]
    my_src = tile_src[0]
    tile_total = tile_count[0]
    my_send = send_rows[0]
    section_count = my_send.shape[0]
    halo_width = my_send.shape[1]
    vert_count = lax.axis_size("vert")
    feat_count = lax.axis_size("feat")
    col_width = row_count // feat_count
    width = weight.shape[1]
    src_blocks = (row_count + section_count * halo_width) // block_size
    norm_scale = 1.0 / math.sqrt(vert_count * row_count)

    def to_blocks(x):
        return x.reshape(channels, feat_count, col_width).transpose(1, 0, 2)

    def from_blocks(x):
        return x.transpose(1, 0, 2).reshape(channels, row_count)

    state_count = states.shape[0]
    pick = (
        jnp.arange(row_count, dtype=jnp.int32)[:, None] == my_send.reshape(-1)[None, :]
    ).astype(bf16)
    listed = jnp.dot(
        states.reshape(state_count * channels, row_count), pick, preferred_element_type=f32
    ).astype(bf16)
    halo_states = lax.all_to_all(
        listed.reshape(state_count, channels, section_count, halo_width),
        "vert",
        split_axis=2,
        concat_axis=2,
        tiled=True,
    )
    mixed_state = jnp.sum(depth_weight[:, :, None] * states, axis=0).astype(bf16)
    mixed_halo = jnp.sum(depth_weight[:, :, None, None] * halo_states, axis=0).astype(bf16)
    extended = jnp.concatenate([mixed_state, mixed_halo.reshape(channels, -1)], axis=1)
    extended = extended.reshape(channels, src_blocks, block_size)
    aggregated = over_tiles(
        tile_forward, extended, my_tiles, my_dst, my_src, tile_total, row_blocks
    )
    aggregated = aggregated.reshape(channels, row_count).astype(bf16)

    bias_cols = jnp.broadcast_to(
        jnp.stack(bf16_parts(bias_vec, 3), axis=1)[None], (feat_count, channels, 3)
    )
    first_send = jnp.concatenate([to_blocks(aggregated), to_blocks(cotangent), bias_cols], axis=2)
    first_recv = lax.all_to_all(first_send, "feat", split_axis=0, concat_axis=0, tiled=True)
    first_recv = first_recv.reshape(feat_count * channels, -1)
    agg_block = first_recv[:, :col_width]
    cot_block = first_recv[:, col_width : 2 * col_width].astype(f32)
    bias_full = parts_sum([first_recv[:, 2 * col_width + n] for n in range(3)])

    pre_act = lax.dot_general(
        weight, agg_block, (((0,), (0,)), ((), ())), preferred_element_type=f32
    )
    pre_act = pre_act + bias_full[:, None]
    sigmoid_pre = jax.nn.sigmoid(pre_act)
    out_block = (pre_act * sigmoid_pre).astype(bf16)
    grad_pre = (cot_block * sigmoid_pre * (1.0 + pre_act * (1.0 - sigmoid_pre))).astype(bf16)
    grad_agg_block = jnp.dot(weight, grad_pre, preferred_element_type=f32).astype(bf16)
    weight_terms = lax.dot_general(
        agg_block, grad_pre, (((1,), (1,)), ((), ())), preferred_element_type=f32
    )
    bias_terms = jnp.sum(grad_pre.astype(f32), axis=1)

    second_send = jnp.concatenate(
        [
            out_block.reshape(feat_count, channels, col_width),
            grad_agg_block.reshape(feat_count, channels, col_width),
            weight_terms.reshape(feat_count, channels, width).astype(bf16),
        ]
        + bf16_parts(bias_terms.reshape(feat_count, channels, 1), 2),
        axis=2,
    )
    second_recv = lax.all_to_all(second_send, "feat", split_axis=0, concat_axis=0, tiled=True)
    layer_out = from_blocks(second_recv[:, :, :col_width])
    grad_agg = from_blocks(second_recv[:, :, col_width : 2 * col_width])
    start = 2 * col_width
    weight_part = second_recv[:, :, start : start + width].astype(f32)
    bias_part = parts_sum(
        [second_recv[:, :, start + width : start + width + 1], second_recv[:, :, start + width + 1 :]]
    )
    panel_terms = jnp.sum(jnp.concatenate([weight_part, bias_part], axis=2), axis=0)

    grad_blocks = grad_agg.reshape(channels, row_blocks, block_size)
    spread_out = over_tiles(
        tile_backward, grad_blocks, my_tiles, my_dst, my_src, tile_total, src_blocks
    )
    spread_out = spread_out.reshape(channels, src_blocks * block_size)
    own_grad = spread_out[:, :row_count]
    halo_part = spread_out[:, row_count:].reshape(channels, section_count, halo_width)
    halo_terms = lax.reduce_precision(halo_part, exponent_bits=8, mantissa_bits=7)
    depth_terms = jnp.sum(states * own_grad[None], axis=2) + jnp.sum(
        halo_states * halo_terms[None], axis=(2, 3)
    )
    weight_total = panel_terms[:, :width].reshape(-1) * norm_scale
    small_total = (
        jnp.concatenate([panel_terms[:, width], depth_terms.reshape(-1)]) * norm_scale
    )
    last_send = jnp.concatenate(
        [halo_part.astype(bf16).transpose(1, 0, 2).reshape(section_count, channels * halo_width)]
        + [
            jnp.broadcast_to(part[None, :], (vert_count, part.shape[0]))
            for part in [weight_total.astype(bf16)] + bf16_parts(small_total, 2)
        ],
        axis=1,
    )
    last_recv = lax.all_to_all(last_send, "vert", split_axis=0, concat_axis=0, tiled=True)
    returned = (
        last_recv[:, : channels * halo_width]
        .reshape(section_count, channels, halo_width)
        .transpose(1, 0, 2)
    )
    tail = last_recv[:, channels * halo_width :]
    weight_count = weight_total.shape[0]
    small_count = small_total.shape[0]
    weight_sum = jnp.sum(tail[:, :weight_count].astype(f32), axis=0)
    small_sum = jnp.sum(
        parts_sum(
            [
                tail[:, weight_count : weight_count + small_count],
                tail[:, weight_count + small_count :],
            ]
        ),
        axis=0,
    )
    hot = (
        my_send.reshape(-1)[:, None] == jnp.arange(row_count, dtype=jnp.int32)[None, :]
    ).astype(bf16)
    added = jnp.dot(returned.reshape(channels, -1), hot, preferred_element_type=f32)
    grad_mixed = own_grad + added
    grad_states = (depth_weight[:, :, None] * grad_mixed[None]).astype(bf16)
    return (
        layer_out,
        grad_states,
        weight_sum.reshape(channels, width),
        small_sum[:channels],
        small_sum[channels:].reshape(depth_terms.shape),
    )


def solution(mesh):
    placed = (
        P(None, "feat", "vert"),
        P(None, "feat"),
        P("vert", None, None, None),
        P("vert", None),
        P("vert", None),
        P("vert"),
        P("vert", None, None),
        P(),
        P("feat"),
        P("feat", "vert"),
    )
    return jax.shard_map(
        local,
        mesh=mesh,
        in_specs=placed,
        out_specs=(
            P("feat", "vert"),
            P(None, "feat", "vert"),
            P("feat", None),
            P("feat"),
            P(None, "feat"),
        ),
        check_vma=False,
    )
```

```python
import math

import jax
import jax.numpy as jnp
from jax import lax
from jax.sharding import PartitionSpec as P


def tile_forward(extended, tile_grp, dst_grp, src_grp, live_mask, row_blocks):
    picked = extended.at[:, src_grp].get(mode="promise_in_bounds")
    products = jnp.einsum("dtc,trc->dtr", picked, tile_grp, preferred_element_type=jnp.float32)
    onehot = (
        (dst_grp[:, None] == jnp.arange(row_blocks, dtype=jnp.int32)[None, :]) & live_mask[:, None]
    ).astype(jnp.float32)
    return jnp.einsum("dtr,tn->dnr", products, onehot)


def tile_backward(grad_blocks, tile_grp, dst_grp, src_grp, live_mask, src_blocks):
    picked = grad_blocks.at[:, dst_grp].get(mode="promise_in_bounds")
    products = jnp.einsum("dtr,trc->dtc", picked, tile_grp, preferred_element_type=jnp.float32)
    onehot = (
        (src_grp[:, None] == jnp.arange(src_blocks, dtype=jnp.int32)[None, :]) & live_mask[:, None]
    ).astype(jnp.float32)
    return jnp.einsum("dtc,ts->dsc", products, onehot)


def over_tiles(kernel, source, tile_values, tile_dst, tile_src, tile_total, out_blocks):
    capacity = tile_values.shape[0]
    live_mask = jnp.arange(capacity, dtype=jnp.int32) < tile_total
    return kernel(source, tile_values, tile_dst, tile_src, live_mask, out_blocks)


def bf16_parts(x, count):
    parts = []
    rest = x
    for _ in range(count - 1):
        head = lax.reduce_precision(rest, exponent_bits=8, mantissa_bits=7)
        parts.append(head.astype(jnp.bfloat16))
        rest = rest - head
    parts.append(rest.astype(jnp.bfloat16))
    return parts


def parts_sum(parts):
    total = parts[0].astype(jnp.float32)
    for part in parts[1:]:
        total = total + part.astype(jnp.float32)
    return total


def local(
    states,
    depth_weight,
    tile_values,
    tile_dst,
    tile_src,
    tile_count,
    send_rows,
    weight,
    bias_vec,
    cotangent,
):
    f32 = jnp.float32
    bf16 = jnp.bfloat16
    channels = states.shape[1]
    row_count = states.shape[2]
    block_size = tile_values.shape[2]
    row_blocks = row_count // block_size
    my_tiles = tile_values[0]
    my_dst = tile_dst[0]
    my_src = tile_src[0]
    tile_total = tile_count[0]
    my_send = send_rows[0]
    section_count = my_send.shape[0]
    halo_width = my_send.shape[1]
    vert_count = lax.axis_size("vert")
    feat_count = lax.axis_size("feat")
    col_width = row_count // feat_count
    width = weight.shape[1]
    src_blocks = (row_count + section_count * halo_width) // block_size
    norm_scale = 1.0 / math.sqrt(vert_count * row_count)

    def to_blocks(x):
        return x.reshape(channels, feat_count, col_width).transpose(1, 0, 2)

    def from_blocks(x):
        return x.transpose(1, 0, 2).reshape(channels, row_count)

    state_count = states.shape[0]
    pick = (
        jnp.arange(row_count, dtype=jnp.int32)[:, None] == my_send.reshape(-1)[None, :]
    ).astype(bf16)
    listed = jnp.dot(
        states.reshape(state_count * channels, row_count), pick, preferred_element_type=f32
    ).astype(bf16)
    halo_states = lax.all_to_all(
        listed.reshape(state_count, channels, section_count, halo_width),
        "vert",
        split_axis=2,
        concat_axis=2,
        tiled=True,
    )
    mixed_state = jnp.sum(depth_weight[:, :, None] * states, axis=0).astype(bf16)
    mixed_halo = jnp.sum(depth_weight[:, :, None, None] * halo_states, axis=0).astype(bf16)
    extended = jnp.concatenate([mixed_state, mixed_halo.reshape(channels, -1)], axis=1)
    extended = extended.reshape(channels, src_blocks, block_size)
    aggregated = over_tiles(
        tile_forward, extended, my_tiles, my_dst, my_src, tile_total, row_blocks
    )
    aggregated = aggregated.reshape(channels, row_count).astype(bf16)

    bias_row = jnp.stack(bf16_parts(bias_vec, 3), axis=1).reshape(-1)
    bias_row = jnp.pad(bias_row, (0, 2 * col_width - bias_row.shape[0]))
    first_send = jnp.concatenate(
        [
            jnp.concatenate([to_blocks(aggregated), to_blocks(cotangent)], axis=2),
            jnp.broadcast_to(bias_row[None, None, :], (feat_count, 1, 2 * col_width)),
        ],
        axis=1,
    )
    first_recv = lax.all_to_all(first_send, "feat", split_axis=0, concat_axis=0, tiled=True)
    block_rows = first_recv[:, :channels, :].reshape(feat_count * channels, -1)
    agg_block = block_rows[:, :col_width]
    cot_block = block_rows[:, col_width:].astype(f32)
    bias_parts = first_recv[:, channels, : channels * 3].reshape(feat_count * channels, 3)
    bias_full = parts_sum([bias_parts[:, n] for n in range(3)])

    pre_act = lax.dot_general(
        weight, agg_block, (((0,), (0,)), ((), ())), preferred_element_type=f32
    )
    pre_act = pre_act + bias_full[:, None]
    sigmoid_pre = jax.nn.sigmoid(pre_act)
    out_block = (pre_act * sigmoid_pre).astype(bf16)
    grad_pre = (cot_block * sigmoid_pre * (1.0 + pre_act * (1.0 - sigmoid_pre))).astype(bf16)
    grad_agg_block = jnp.dot(weight, grad_pre, preferred_element_type=f32).astype(bf16)
    weight_terms = lax.dot_general(
        agg_block, grad_pre, (((1,), (1,)), ((), ())), preferred_element_type=f32
    )
    bias_terms = jnp.sum(grad_pre.astype(f32), axis=1)

    second_send = jnp.concatenate(
        [
            out_block.reshape(feat_count, channels, col_width),
            grad_agg_block.reshape(feat_count, channels, col_width),
            weight_terms.reshape(feat_count, channels, width).astype(bf16),
        ]
        + bf16_parts(bias_terms.reshape(feat_count, channels, 1), 2),
        axis=2,
    )
    second_recv = lax.all_to_all(second_send, "feat", split_axis=0, concat_axis=0, tiled=True)
    layer_out = from_blocks(second_recv[:, :, :col_width])
    grad_agg = from_blocks(second_recv[:, :, col_width : 2 * col_width])
    start = 2 * col_width
    weight_part = second_recv[:, :, start : start + width].astype(f32)
    bias_part = parts_sum(
        [second_recv[:, :, start + width : start + width + 1], second_recv[:, :, start + width + 1 :]]
    )
    panel_terms = jnp.sum(jnp.concatenate([weight_part, bias_part], axis=2), axis=0)

    grad_blocks = grad_agg.reshape(channels, row_blocks, block_size)
    spread_out = over_tiles(
        tile_backward, grad_blocks, my_tiles, my_dst, my_src, tile_total, src_blocks
    )
    spread_out = spread_out.reshape(channels, src_blocks * block_size)
    own_grad = spread_out[:, :row_count]
    halo_part = spread_out[:, row_count:].reshape(channels, section_count, halo_width)
    halo_terms = lax.reduce_precision(halo_part, exponent_bits=8, mantissa_bits=7)
    depth_terms = jnp.sum(states * own_grad[None], axis=2) + jnp.sum(
        halo_states * halo_terms[None], axis=(2, 3)
    )
    weight_total = panel_terms[:, :width].reshape(-1) * norm_scale
    small_total = (
        jnp.concatenate([panel_terms[:, width], depth_terms.reshape(-1)]) * norm_scale
    )
    last_send = jnp.concatenate(
        [halo_part.astype(bf16).transpose(1, 0, 2).reshape(section_count, channels * halo_width)]
        + [
            jnp.broadcast_to(part[None, :], (vert_count, part.shape[0]))
            for part in [weight_total.astype(bf16)] + bf16_parts(small_total, 2)
        ],
        axis=1,
    )
    last_recv = lax.all_to_all(last_send, "vert", split_axis=0, concat_axis=0, tiled=True)
    returned = (
        last_recv[:, : channels * halo_width]
        .reshape(section_count, channels, halo_width)
        .transpose(1, 0, 2)
    )
    tail = last_recv[:, channels * halo_width :]
    weight_count = weight_total.shape[0]
    small_count = small_total.shape[0]
    weight_sum = jnp.sum(tail[:, :weight_count].astype(f32), axis=0)
    small_sum = jnp.sum(
        parts_sum(
            [
                tail[:, weight_count : weight_count + small_count],
                tail[:, weight_count + small_count :],
            ]
        ),
        axis=0,
    )
    hot = (
        my_send.reshape(-1)[None, :] == jnp.arange(row_count, dtype=jnp.int32)[:, None]
    ).astype(bf16)
    added = lax.dot_general(
        hot,
        returned.reshape(channels, -1),
        (((1,), (1,)), ((), ())),
        preferred_element_type=f32,
    )
    grad_mixed = own_grad + added.T
    grad_states = (depth_weight[:, :, None] * grad_mixed[None]).astype(bf16)
    return (
        layer_out,
        grad_states,
        weight_sum.reshape(channels, width),
        small_sum[:channels],
        small_sum[channels:].reshape(depth_terms.shape),
    )


def solution(mesh):
    placed = (
        P(None, "feat", "vert"),
        P(None, "feat"),
        P("vert", None, None, None),
        P("vert", None),
        P("vert", None),
        P("vert"),
        P("vert", None, None),
        P(),
        P("feat"),
        P("feat", "vert"),
    )
    return jax.shard_map(
        local,
        mesh=mesh,
        in_specs=placed,
        out_specs=(
            P("feat", "vert"),
            P(None, "feat", "vert"),
            P("feat", None),
            P("feat"),
            P(None, "feat"),
        ),
        check_vma=False,
    )
```

```python
import math

import jax
import jax.numpy as jnp
from jax import lax
from jax.sharding import PartitionSpec as P


def tile_forward(extended, tile_grp, dst_grp, src_grp, live_mask, row_blocks):
    picked = extended.at[:, src_grp].get(mode="promise_in_bounds")
    products = jnp.einsum("dtc,trc->dtr", picked, tile_grp, preferred_element_type=jnp.float32)
    onehot = (
        (dst_grp[:, None] == jnp.arange(row_blocks, dtype=jnp.int32)[None, :]) & live_mask[:, None]
    ).astype(jnp.float32)
    return jnp.einsum("dtr,tn->dnr", products, onehot)


def tile_backward(grad_blocks, tile_grp, dst_grp, src_grp, live_mask, src_blocks):
    picked = grad_blocks.at[:, dst_grp].get(mode="promise_in_bounds")
    products = jnp.einsum("dtr,trc->dtc", picked, tile_grp, preferred_element_type=jnp.float32)
    onehot = (
        (src_grp[:, None] == jnp.arange(src_blocks, dtype=jnp.int32)[None, :]) & live_mask[:, None]
    ).astype(jnp.float32)
    return jnp.einsum("dtc,ts->dsc", products, onehot)


def over_tiles(kernel, source, tile_values, tile_dst, tile_src, tile_total, out_blocks):
    capacity = tile_values.shape[0]
    live_mask = jnp.arange(capacity, dtype=jnp.int32) < tile_total
    return kernel(source, tile_values, tile_dst, tile_src, live_mask, out_blocks)


def bf16_parts(x, count):
    parts = []
    rest = x
    for _ in range(count - 1):
        head = lax.reduce_precision(rest, exponent_bits=8, mantissa_bits=7)
        parts.append(head.astype(jnp.bfloat16))
        rest = rest - head
    parts.append(rest.astype(jnp.bfloat16))
    return parts


def parts_sum(parts):
    total = parts[0].astype(jnp.float32)
    for part in parts[1:]:
        total = total + part.astype(jnp.float32)
    return total


def local(
    states,
    depth_weight,
    tile_values,
    tile_dst,
    tile_src,
    tile_count,
    send_rows,
    weight,
    bias_vec,
    cotangent,
):
    f32 = jnp.float32
    bf16 = jnp.bfloat16
    channels = states.shape[1]
    row_count = states.shape[2]
    block_size = tile_values.shape[2]
    row_blocks = row_count // block_size
    my_tiles = tile_values[0]
    my_dst = tile_dst[0]
    my_src = tile_src[0]
    tile_total = tile_count[0]
    my_send = send_rows[0]
    section_count = my_send.shape[0]
    halo_width = my_send.shape[1]
    vert_count = lax.axis_size("vert")
    feat_count = lax.axis_size("feat")
    col_width = row_count // feat_count
    width = weight.shape[1]
    src_blocks = (row_count + section_count * halo_width) // block_size
    norm_scale = 1.0 / math.sqrt(vert_count * row_count)

    def to_blocks(x):
        return x.reshape(channels, feat_count, col_width).transpose(1, 0, 2)

    def from_blocks(x):
        return x.transpose(1, 0, 2).reshape(channels, row_count)

    state_count = states.shape[0]
    pick = (
        jnp.arange(row_count, dtype=jnp.int32)[:, None] == my_send.reshape(-1)[None, :]
    ).astype(bf16)
    listed = jnp.dot(
        states.reshape(state_count * channels, row_count), pick, preferred_element_type=f32
    ).astype(bf16)
    halo_states = lax.all_to_all(
        listed.reshape(state_count, channels, section_count, halo_width),
        "vert",
        split_axis=2,
        concat_axis=2,
        tiled=True,
    )
    mixed_state = jnp.sum(depth_weight[:, :, None] * states, axis=0).astype(bf16)
    mixed_halo = jnp.sum(depth_weight[:, :, None, None] * halo_states, axis=0).astype(bf16)
    extended = jnp.concatenate([mixed_state, mixed_halo.reshape(channels, -1)], axis=1)
    extended = extended.reshape(channels, src_blocks, block_size)
    aggregated = over_tiles(
        tile_forward, extended, my_tiles, my_dst, my_src, tile_total, row_blocks
    )
    aggregated = aggregated.reshape(channels, row_count).astype(bf16)

    bias_cols = jnp.broadcast_to(
        jnp.stack(bf16_parts(bias_vec, 3), axis=1)[None], (feat_count, channels, 3)
    )
    first_send = jnp.concatenate([to_blocks(aggregated), to_blocks(cotangent), bias_cols], axis=2)
    first_recv = lax.all_to_all(first_send, "feat", split_axis=0, concat_axis=0, tiled=True)
    first_recv = first_recv.reshape(feat_count * channels, -1)
    agg_block = first_recv[:, :col_width]
    cot_block = first_recv[:, col_width : 2 * col_width].astype(f32)
    bias_full = parts_sum([first_recv[:, 2 * col_width + n] for n in range(3)])

    pre_act = lax.dot_general(
        weight, agg_block, (((0,), (0,)), ((), ())), preferred_element_type=f32
    )
    pre_act = pre_act + bias_full[:, None]
    sigmoid_pre = jax.nn.sigmoid(pre_act)
    out_block = (pre_act * sigmoid_pre).astype(bf16)
    grad_pre = (cot_block * sigmoid_pre * (1.0 + pre_act * (1.0 - sigmoid_pre))).astype(bf16)
    grad_agg_block = jnp.dot(weight, grad_pre, preferred_element_type=f32).astype(bf16)
    weight_terms = lax.dot_general(
        agg_block, grad_pre, (((1,), (1,)), ((), ())), preferred_element_type=f32
    )
    bias_terms = jnp.sum(grad_pre.astype(f32), axis=1)

    main_cols = 2 * col_width + width
    bias_row = jnp.concatenate(bf16_parts(bias_terms.reshape(feat_count, channels), 2), axis=1)
    bias_row = jnp.pad(bias_row, ((0, 0), (0, main_cols - 2 * channels)))
    second_send = jnp.concatenate(
        [
            jnp.concatenate(
                [
                    out_block.reshape(feat_count, channels, col_width),
                    grad_agg_block.reshape(feat_count, channels, col_width),
                    weight_terms.reshape(feat_count, channels, width).astype(bf16),
                ],
                axis=2,
            ),
            bias_row[:, None, :],
        ],
        axis=1,
    )
    second_recv = lax.all_to_all(second_send, "feat", split_axis=0, concat_axis=0, tiled=True)
    layer_out = from_blocks(second_recv[:, :channels, :col_width])
    grad_agg = from_blocks(second_recv[:, :channels, col_width : 2 * col_width])
    start = 2 * col_width
    weight_part = second_recv[:, :channels, start : start + width].astype(f32)
    bias_part = parts_sum(
        [
            second_recv[:, channels, :channels],
            second_recv[:, channels, channels : 2 * channels],
        ]
    )[:, :, None]
    panel_terms = jnp.sum(jnp.concatenate([weight_part, bias_part], axis=2), axis=0)

    grad_blocks = grad_agg.reshape(channels, row_blocks, block_size)
    spread_out = over_tiles(
        tile_backward, grad_blocks, my_tiles, my_dst, my_src, tile_total, src_blocks
    )
    spread_out = spread_out.reshape(channels, src_blocks * block_size)
    own_grad = spread_out[:, :row_count]
    halo_part = spread_out[:, row_count:].reshape(channels, section_count, halo_width)
    halo_terms = lax.reduce_precision(halo_part, exponent_bits=8, mantissa_bits=7)
    depth_terms = jnp.sum(states * own_grad[None], axis=2) + jnp.sum(
        halo_states * halo_terms[None], axis=(2, 3)
    )
    weight_total = panel_terms[:, :width].reshape(-1) * norm_scale
    small_total = (
        jnp.concatenate([panel_terms[:, width], depth_terms.reshape(-1)]) * norm_scale
    )
    last_send = jnp.concatenate(
        [halo_part.astype(bf16).transpose(1, 0, 2).reshape(section_count, channels * halo_width)]
        + [
            jnp.broadcast_to(part[None, :], (vert_count, part.shape[0]))
            for part in [weight_total.astype(bf16)] + bf16_parts(small_total, 2)
        ],
        axis=1,
    )
    last_recv = lax.all_to_all(last_send, "vert", split_axis=0, concat_axis=0, tiled=True)
    returned = (
        last_recv[:, : channels * halo_width]
        .reshape(section_count, channels, halo_width)
        .transpose(1, 0, 2)
    )
    tail = last_recv[:, channels * halo_width :]
    weight_count = weight_total.shape[0]
    small_count = small_total.shape[0]
    weight_sum = jnp.sum(tail[:, :weight_count].astype(f32), axis=0)
    small_sum = jnp.sum(
        parts_sum(
            [
                tail[:, weight_count : weight_count + small_count],
                tail[:, weight_count + small_count :],
            ]
        ),
        axis=0,
    )
    hot = (
        my_send.reshape(-1)[None, :] == jnp.arange(row_count, dtype=jnp.int32)[:, None]
    ).astype(bf16)
    added = lax.dot_general(
        hot,
        returned.reshape(channels, -1),
        (((1,), (1,)), ((), ())),
        preferred_element_type=f32,
    )
    grad_mixed = own_grad + added.T
    grad_states = (depth_weight[:, :, None] * grad_mixed[None]).astype(bf16)
    return (
        layer_out,
        grad_states,
        weight_sum.reshape(channels, width),
        small_sum[:channels],
        small_sum[channels:].reshape(depth_terms.shape),
    )


def solution(mesh):
    placed = (
        P(None, "feat", "vert"),
        P(None, "feat"),
        P("vert", None, None, None),
        P("vert", None),
        P("vert", None),
        P("vert"),
        P("vert", None, None),
        P(),
        P("feat"),
        P("feat", "vert"),
    )
    return jax.shard_map(
        local,
        mesh=mesh,
        in_specs=placed,
        out_specs=(
            P("feat", "vert"),
            P(None, "feat", "vert"),
            P("feat", None),
            P("feat"),
            P(None, "feat"),
        ),
        check_vma=False,
    )
```
